256 devices in a mesh: grp: 8 (over x, core), cell: 32 (over y, z).
Axes of the slice: x: 4, y: 4, z: 8, core: 2. Of those that a mesh axis runs over, the one named last changes fastest.
Arguments:
- rhs: float32 [128, 2, 128, 16, 128], P('grp', None, 'cell'), may hold values from -8 to 8
- log_perm: float32 [128, 128, 16, 128], P('grp', 'cell'), may hold values from -1.5 to 1.5
- porosity: float32 [128, 128, 16, 128], P('grp', 'cell'), may hold values from 0.1 to 0.3
- saturation: float32 [128, 128, 16, 128], P('grp', 'cell'), may hold values from 0.2 to 0.8
- pressure: float32 [128, 128, 16, 128], P('grp', 'cell'), may hold values from -6 to 6
- obs_values: float32 [256], replicated, may hold values from -6 to 6
- obs_error: float32 [256], replicated, may hold values from 0.1 to 1
- noise: float32 [128, 256], replicated, may hold values from -6 to 6
- well_cell: int32 [128], replicated, may hold values from 0 to 262143
- obs_well: int32 [256], replicated, may hold values from 0 to 127
Outputs:
- increment: float32 [128, 2, 128, 16, 128], P('grp', None, 'cell')
- log_perm_post: float32 [128, 128, 16, 128], P('grp', 'cell')
- porosity_post: float32 [128, 128, 16, 128], P('grp', 'cell')
The draws below stay inside these ranges and needn't reach their ends.
All inputs are finite; a program needn't handle non-finite values.
Results may differ from the reference program's by a relative error of at most 0.0003.
Values sent between devices are 32-bit elements; how exact they have to be, the bound alone decides.
No kernel may reach another device: no remote copies, remote signals or barrier semaphores. Data moves between devices by JAX's collectives and lax.ppermute only.
A program may use at most 128 MiB of HBM per device.

```python
import math
import jax
import jax.numpy as jnp
from jax import lax

NY = 16
NZ = 128
KRYLOV = 4
NWELL = 128
NOBS = 256
MEMBERS = 128
NX = 128


def draw_rhs(key, part):
    shape = (MEMBERS, 2, NX, NY, NZ)
    position = jnp.arange(NX, dtype=jnp.float32) / max(NX - 1, 1)
    ramp = (1.0 + 2.0 * position)[None, None, :, None, None]
    values = jax.random.normal(key, shape, jnp.float32) * ramp
    return jnp.clip(values, -8.0, 8.0)


def with_ends(values, own_key, smallest, largest):
    longest = values.shape.index(max(values.shape))
    spots = []
    for shift in (0, 1):
        where = [jax.random.randint(jax.random.fold_in(own_key, axis), (), 0, length) for axis, length in enumerate(values.shape)]
        where[longest] = (where[longest] + shift) % values.shape[longest]
        spots.append(tuple(where))
    return values.at[spots[0]].set(smallest).at[spots[1]].set(largest)


def block_levels(own_key, extent, pieces, smallest, largest):
    factor_of, own = 1.0, jax.random.fold_in(own_key, 6)
    for axis_at, shards_of in pieces:
        steps = jnp.exp(jax.random.uniform(jax.random.fold_in(own, axis_at), (shards_of,), jnp.float32, smallest / len(pieces), largest / len(pieces)))
        factor_of = factor_of * jnp.repeat(steps, extent[axis_at] // shards_of).reshape([-1 if axis == axis_at else 1 for axis in range(len(extent))])
    return factor_of


def normal_values(own_key, extent, width, reach, split=(), held_as=jnp.bfloat16):
    factor_of = block_levels(own_key, extent, split, -0.22, 0.18) if split else 1.0
    drawn = jax.random.normal(own_key, extent, jnp.float32) * width * factor_of
    return jnp.minimum(jnp.maximum(drawn, -reach), reach).astype(held_as)


def setup_inputs(seed: int = 0) -> dict:
    keys = jax.random.split(jax.random.key(seed), 11)
    return {
        "rhs": draw_rhs(jax.random.fold_in(keys[10], 71), 0),
        "log_perm": jnp.clip(jax.random.uniform(keys[1], (MEMBERS, NX, NY, NZ), jnp.float32, -1.5, 1.5) * block_levels(keys[1], (MEMBERS, NX, NY, NZ), ((0, 8), (1, 32)), -0.4, 0.0), -1.5, 1.5),
        "porosity": jnp.clip(0.1 + 0.20000001043081284 * jax.random.uniform(keys[2], (MEMBERS, NX, NY, NZ), jnp.float32) ** block_levels(keys[2], (MEMBERS, NX, NY, NZ), ((0, 8), (1, 32)), -0.2, 0.2), 0.1, 0.3),
        "saturation": jnp.clip(0.2 + 0.6 * jax.random.uniform(keys[3], (MEMBERS, NX, NY, NZ), jnp.float32) ** block_levels(keys[3], (MEMBERS, NX, NY, NZ), ((0, 8), (1, 32)), -0.2, 0.2), 0.2, 0.8),
        "pressure": normal_values(keys[4], (MEMBERS, NX, NY, NZ), 1.0, 6.0, ((0, 8), (1, 32)), jnp.float32),
        "obs_values": normal_values(keys[5], (NOBS,), 1.0, 6.0, (), jnp.float32),
        "obs_error": jnp.clip(jnp.exp(jax.random.uniform(keys[6], (NOBS,), jnp.float32, math.log(0.1), math.log(1.0))), 0.1, 1.0),
        "noise": normal_values(keys[7], (MEMBERS, NOBS), 1.0, 6.0, (), jnp.float32),
        "well_cell": with_ends(jax.random.randint(keys[8], (NWELL,), 0, NX * NY * NZ), jax.random.fold_in(keys[8], 1), 0, (NX * NY * NZ) - 1).astype(jnp.int32),
        "obs_well": with_ends(jax.random.randint(keys[9], (NOBS,), 0, NWELL), jax.random.fold_in(keys[9], 1), 0, NWELL - 1).astype(jnp.int32),
    }


epsilon = 1e-06
time_step = 0.1
compress = 0.5
inflation = 4.0

def mobility(sat_field):
    return sat_field * sat_field + 0.5 * (1.0 - sat_field) * (1.0 - sat_field)

def face_pair(perm_low, perm_high, sat_low, sat_high):
    trans = 2.0 * perm_low * perm_high / (perm_low + perm_high) * (0.5 * (mobility(sat_low) + mobility(sat_high)))
    return (trans, trans * (0.5 * (sat_low + sat_high)))

def plane_faces(perm, sat_field):
    plane_rows = perm.shape[-2]
    plane_cols = perm.shape[-1]
    keep_rows = (lax.broadcasted_iota(jnp.int32, (plane_rows, plane_cols), 0) < plane_rows - 1).astype(jnp.float32)
    keep_cols = (lax.broadcasted_iota(jnp.int32, (plane_rows, plane_cols), 1) < plane_cols - 1).astype(jnp.float32)
    trans_y, frac_y = face_pair(perm, jnp.roll(perm, -1, -2), sat_field, jnp.roll(sat_field, -1, -2))
    trans_z, frac_z = face_pair(perm, jnp.roll(perm, -1, -1), sat_field, jnp.roll(sat_field, -1, -1))
    return (trans_y * keep_rows, frac_y * keep_rows, trans_z * keep_cols, frac_z * keep_cols)

def operator(padded, second, coeffs):
    accum, trans_x, frac_x, trans_y, frac_y, trans_z, frac_z = coeffs
    first = padded[..., 1:-1, :, :]
    diff_x = padded[..., 1:, :, :] - padded[..., :-1, :, :]
    diff_y = jnp.roll(first, -1, -2) - first
    diff_z = jnp.roll(first, -1, -1) - first

    def net(coef_x, coef_y, coef_z):
        flow_x = coef_x * diff_x
        flow_y = coef_y * diff_y
        flow_z = coef_z * diff_z
        return flow_x[..., :-1, :, :] - flow_x[..., 1:, :, :] + (jnp.roll(flow_y, 1, -2) - flow_y) + (jnp.roll(flow_z, 1, -1) - flow_z)
    out_pressure = accum * (compress * first + 0.5 * second) + net(trans_x, trans_y, trans_z)
    out_water = accum * second + net(frac_x, frac_y, frac_z)
    return (out_pressure, out_water)

def least_squares(columns, beta):
    rows = [list(column) for column in columns]
    cosines = []
    sines = []
    target = [beta] + [jnp.zeros_like(beta) for column in columns]
    for jdx in range(len(rows)):
        column = rows[jdx]
        for idx in range(jdx):
            upper = cosines[idx] * column[idx] + sines[idx] * column[idx + 1]
            column[idx + 1] = -sines[idx] * column[idx] + cosines[idx] * column[idx + 1]
            column[idx] = upper
        radius = jnp.sqrt(column[jdx] * column[jdx] + column[jdx + 1] * column[jdx + 1])
        cosines.append(column[jdx] / radius)
        sines.append(column[jdx + 1] / radius)
        column[jdx] = radius
        target[jdx + 1] = -sines[jdx] * target[jdx]
        target[jdx] = cosines[jdx] * target[jdx]
    count = len(rows)
    solved = [None] * count
    for jdx in reversed(range(count)):
        partial_sum = target[jdx]
        for idx in range(jdx + 1, count):
            partial_sum = partial_sum - rows[idx][jdx] * solved[idx]
        solved[jdx] = partial_sum / rows[jdx][jdx]
    return solved

def member_coeffs(lperm, sat_field, poro):
    perm = jnp.exp(lperm)
    trans_x, frac_x = face_pair(perm[:-1], perm[1:], sat_field[:-1], sat_field[1:])
    trans_x = jnp.pad(trans_x, ((1, 1), (0, 0), (0, 0)))
    frac_x = jnp.pad(frac_x, ((1, 1), (0, 0), (0, 0)))
    trans_y, frac_y, trans_z, frac_z = plane_faces(perm, sat_field)
    return (poro / time_step, trans_x, frac_x, trans_y, frac_y, trans_z, frac_z)

def solve_member(inputs):
    rhs_member, lperm, sat_field, poro = inputs
    coeffs = member_coeffs(lperm, sat_field, poro)

    def inner(left, right):
        return jnp.sum(left * right)

    def apply(vector):
        padded = jnp.pad(vector[0], ((1, 1), (0, 0), (0, 0)))
        out_pressure, out_water = operator(padded, vector[1], coeffs)
        return jnp.stack([out_pressure, out_water], 0)
    beta = jnp.sqrt(inner(rhs_member, rhs_member) + epsilon)
    basis = [rhs_member / beta]
    columns = []
    for jdx in range(KRYLOV):
        image = apply(basis[jdx])
        projected = [inner(basis[idx], image) for idx in range(jdx + 1)]
        for idx in range(jdx + 1):
            image = image - projected[idx] * basis[idx]
        height = jnp.sqrt(inner(image, image) + epsilon)
        columns.append(projected + [height])
        basis.append(image / height)
    solved = least_squares(columns, beta)
    result = solved[0] * basis[0]
    for jdx in range(1, KRYLOV):
        result = result + solved[jdx] * basis[jdx]
    return result

def ensemble_weights(predicted, obs_values, obs_error, noise):
    members = predicted.shape[0]
    sigma = math.sqrt(inflation) * obs_error
    center = lax.optimization_barrier(jnp.mean(predicted, axis=0))
    spread = (predicted - center) / (math.sqrt(members - 1.0) * sigma)
    innov = (obs_values + sigma * noise - predicted) / sigma
    gram = jnp.eye(members, dtype=jnp.float32) + jnp.dot(spread.astype(jnp.float32), spread.T.astype(jnp.float32), precision=lax.Precision.HIGHEST, preferred_element_type=jnp.float32)
    cross = jnp.dot(spread.astype(jnp.float32), innov.T.astype(jnp.float32), precision=lax.Precision.HIGHEST, preferred_element_type=jnp.float32)
    factor = jnp.linalg.cholesky(gram)
    return jax.scipy.linalg.cho_solve((factor, True), cross)

def reference(rhs, log_perm, porosity, saturation, pressure, obs_values, obs_error, noise, well_cell, obs_well):
    increment = lax.map(solve_member, (rhs, log_perm, saturation, porosity))
    cells_all = NX * NY * NZ
    flat = jnp.stack([pressure + increment[:, 0], saturation + increment[:, 1]], 1).reshape(MEMBERS, 2 * cells_all)
    cells = jnp.take(well_cell, obs_well).astype(jnp.int32)
    component = (jnp.arange(NOBS, dtype=jnp.int32) >= NWELL).astype(jnp.int32)
    predicted = jnp.take(flat, component * cells_all + cells, axis=1)
    weights = ensemble_weights(predicted, obs_values, obs_error, noise)
    params = jnp.stack([log_perm, porosity], 1).reshape(MEMBERS, 2 * cells_all)
    scaled = params / math.sqrt(MEMBERS - 1.0)
    update = jnp.dot(weights.T.astype(jnp.float32), scaled.astype(jnp.float32), precision=lax.Precision.HIGHEST, preferred_element_type=jnp.float32)
    posterior = (params + update).reshape(MEMBERS, 2, NX, NY, NZ)
    return (increment, posterior[:, 0], posterior[:, 1])
```

```python
import math

import jax
import jax.numpy as jnp
from jax import lax
from jax.sharding import Mesh
from jax.sharding import PartitionSpec as P

KRYLOV = 4


epsilon = 1e-06
time_step = 0.1
compress = 0.5
inflation = 4.0


CELL = ("cy", "cz")


def cell_sum(values):
    return lax.psum(lax.psum(values, "cz"), "cy")


def with_halo(block, sides, width):
    for axis, dim in sides:
        count = lax.axis_size(axis[0]) * lax.axis_size(axis[1])
        forward = [(i, i + 1) for i in range(count - 1)]
        backward = [(target, source) for source, target in forward]
        low = lax.ppermute(
            lax.slice_in_dim(block, block.shape[dim] - width, None, axis=dim), axis, forward
        )
        high = lax.ppermute(lax.slice_in_dim(block, 0, width, axis=dim), axis, backward)
        block = jnp.concatenate([low, block, high], axis=dim)
    return block


def mobility(sat_field):
    return sat_field * sat_field + 0.5 * (1.0 - sat_field) * (1.0 - sat_field)


def face_pair(perm_low, perm_high, sat_low, sat_high):
    trans = (
        2.0
        * perm_low
        * perm_high
        / (perm_low + perm_high)
        * (0.5 * (mobility(sat_low) + mobility(sat_high)))
    )
    return (trans, trans * (0.5 * (sat_low + sat_high)))


def plane_faces(perm, sat_field):
    plane_rows = perm.shape[-2]
    plane_cols = perm.shape[-1]
    keep_rows = (
        lax.broadcasted_iota(jnp.int32, (plane_rows, plane_cols), 0) < plane_rows - 1
    ).astype(jnp.float32)
    keep_cols = (
        lax.broadcasted_iota(jnp.int32, (plane_rows, plane_cols), 1) < plane_cols - 1
    ).astype(jnp.float32)
    trans_y, frac_y = face_pair(
        perm, jnp.roll(perm, -1, -2), sat_field, jnp.roll(sat_field, -1, -2)
    )
    trans_z, frac_z = face_pair(
        perm, jnp.roll(perm, -1, -1), sat_field, jnp.roll(sat_field, -1, -1)
    )
    return (trans_y * keep_rows, frac_y * keep_rows, trans_z * keep_cols, frac_z * keep_cols)


def operator(padded, second, coeffs):
    accum, trans_x, frac_x, trans_y, frac_y, trans_z, frac_z = coeffs
    first = padded[..., 1:-1, :, :]
    diff_x = padded[..., 1:, :, :] - padded[..., :-1, :, :]
    diff_y = jnp.roll(first, -1, -2) - first
    diff_z = jnp.roll(first, -1, -1) - first

    def net(coef_x, coef_y, coef_z):
        flow_x = coef_x * diff_x
        flow_y = coef_y * diff_y
        flow_z = coef_z * diff_z
        return (
            flow_x[..., :-1, :, :]
            - flow_x[..., 1:, :, :]
            + (jnp.roll(flow_y, 1, -2) - flow_y)
            + (jnp.roll(flow_z, 1, -1) - flow_z)
        )

    out_pressure = accum * (compress * first + 0.5 * second) + net(trans_x, trans_y, trans_z)
    out_water = accum * second + net(frac_x, frac_y, frac_z)
    return (out_pressure, out_water)


def least_squares(columns, beta):
    rows = [list(column) for column in columns]
    cosines = []
    sines = []
    target = [beta] + [jnp.zeros_like(beta) for column in columns]
    for jdx in range(len(rows)):
        column = rows[jdx]
        for idx in range(jdx):
            upper = cosines[idx] * column[idx] + sines[idx] * column[idx + 1]
            column[idx + 1] = -sines[idx] * column[idx] + cosines[idx] * column[idx + 1]
            column[idx] = upper
        radius = jnp.sqrt(column[jdx] * column[jdx] + column[jdx + 1] * column[jdx + 1])
        cosines.append(column[jdx] / radius)
        sines.append(column[jdx + 1] / radius)
        column[jdx] = radius
        target[jdx + 1] = -sines[jdx] * target[jdx]
        target[jdx] = cosines[jdx] * target[jdx]
    count = len(rows)
    solved = [None] * count
    for jdx in reversed(range(count)):
        partial_sum = target[jdx]
        for idx in range(jdx + 1, count):
            partial_sum = partial_sum - rows[idx][jdx] * solved[idx]
        solved[jdx] = partial_sum / rows[jdx][jdx]
    return solved


def ensemble_weights(predicted, obs_values, obs_error, noise):
    members = predicted.shape[0]
    sigma = math.sqrt(inflation) * obs_error
    center = jnp.mean(predicted, axis=0)
    spread = (predicted - center) / (math.sqrt(members - 1.0) * sigma)
    innov = (obs_values + sigma * noise - predicted) / sigma
    gram = jnp.eye(members, dtype=jnp.float32) + jnp.dot(
        spread, spread.T, precision=lax.Precision.HIGHEST, preferred_element_type=jnp.float32
    )
    cross = jnp.dot(
        spread, innov.T, precision=lax.Precision.HIGHEST, preferred_element_type=jnp.float32
    )
    factor = jnp.linalg.cholesky(gram)
    return jax.scipy.linalg.cho_solve((factor, True), cross)


def expand(values):
    return values[:, None, None, None, None]


def inner(left, right):
    return jnp.sum(left * right, axis=(1, 2, 3, 4))


def local(
    rhs, log_perm, porosity, saturation, pressure, obs_values, obs_error, noise, well_cell, obs_well
):
    local_members, slab_x, plane_rows, plane_cols = log_perm.shape
    members = noise.shape[0]
    plane = plane_rows * plane_cols
    cells_dev = slab_x * plane
    slab_index = lax.axis_index("cy") * lax.axis_size("cz") + lax.axis_index("cz")
    slab_count = lax.axis_size("cy") * lax.axis_size("cz")
    stacked = jnp.stack([log_perm, saturation], axis=1)
    rimmed = with_halo(stacked, ((CELL, 2),), 1)
    perm_pad = jnp.exp(rimmed[:, 0])
    sat_pad = rimmed[:, 1]
    trans_x, frac_x = face_pair(perm_pad[:, :-1], perm_pad[:, 1:], sat_pad[:, :-1], sat_pad[:, 1:])
    face_pos = lax.broadcasted_iota(jnp.int32, (slab_x + 1, 1, 1), 0)
    keep_face = jnp.where(
        face_pos == 0,
        slab_index > 0,
        jnp.where(face_pos == slab_x, slab_index < slab_count - 1, True),
    ).astype(jnp.float32)
    trans_x = trans_x * keep_face
    frac_x = frac_x * keep_face
    trans_y, frac_y, trans_z, frac_z = plane_faces(perm_pad[:, 1:-1], saturation)
    coeffs = (porosity / time_step, trans_x, frac_x, trans_y, frac_y, trans_z, frac_z)
    columns = []
    beta = jnp.sqrt(cell_sum(inner(rhs, rhs)) + epsilon)
    basis = [rhs / expand(beta)]
    for jdx in range(KRYLOV):
        vector = basis[jdx]
        padded = with_halo(vector[:, 0], ((CELL, 1),), 1)
        out_pressure, out_water = operator(padded, vector[:, 1], coeffs)
        image = jnp.stack([out_pressure, out_water], 1)
        local_dots = jnp.stack([inner(basis[idx], image) for idx in range(jdx + 1)], 0)
        projected = cell_sum(local_dots)
        for idx in range(jdx + 1):
            image = image - expand(projected[idx]) * basis[idx]
        height = jnp.sqrt(cell_sum(inner(image, image)) + epsilon)
        columns.append([projected[idx] for idx in range(jdx + 1)] + [height])
        basis.append(image / expand(height))
    solved = least_squares(columns, beta)
    increment = expand(solved[0]) * basis[0]
    for jdx in range(1, KRYLOV):
        increment = increment + expand(solved[jdx]) * basis[jdx]
    flat = jnp.stack([pressure + increment[:, 0], saturation + increment[:, 1]], 1).reshape(
        local_members, 2 * cells_dev
    )
    cells = jnp.take(well_cell, obs_well)
    wells = well_cell.shape[0]
    component = (jnp.arange(obs_well.shape[0], dtype=jnp.int32) >= wells).astype(jnp.int32)
    slab_row = cells // plane - slab_index * slab_x
    inside = (slab_row >= 0) & (slab_row < slab_x)
    local_cell = jnp.where(inside, slab_row * plane + cells % plane, 0)
    picked = jnp.take(flat, component * cells_dev + local_cell, axis=1) * inside.astype(jnp.float32)
    slab_pred = cell_sum(picked)
    predicted = lax.all_gather(slab_pred, "grp", axis=0, tiled=True)
    weights = ensemble_weights(predicted, obs_values, obs_error, noise)
    params = jnp.stack([log_perm, porosity], 1).reshape(local_members, 2 * cells_dev)
    offset = lax.axis_index("grp") * local_members
    scale_factor = 1.0 / math.sqrt(members - 1.0)
    scaled = params * scale_factor
    own_columns = lax.dynamic_slice_in_dim(weights, offset, local_members, 1)
    update = jnp.dot(
        own_columns.T,
        lax.all_gather(scaled, "grp", axis=0, tiled=True),
        precision=lax.Precision.HIGHEST,
        preferred_element_type=jnp.float32,
    )
    posterior = params + update
    posterior = posterior.reshape(local_members, 2, slab_x, plane_rows, plane_cols)
    return (increment, posterior[:, 0], posterior[:, 1])


def split_mesh(mesh):
    devices = mesh.devices
    groups, slabs = devices.shape
    along_z = len({device.coords[2] for device in devices[0]})
    return Mesh(devices.reshape(groups, slabs // along_z, along_z), ("grp", "cy", "cz"))


def solution(mesh):
    mesh = split_mesh(mesh)
    in_specs = (
        P("grp", None, CELL, None, None),
        P("grp", CELL, None, None),
        P("grp", CELL, None, None),
        P("grp", CELL, None, None),
        P("grp", CELL, None, None),
        P(),
        P(),
        P(),
        P(),
        P(),
    )
    out_specs = (
        P("grp", None, CELL, None, None),
        P("grp", CELL, None, None),
        P("grp", CELL, None, None),
    )
    return jax.shard_map(local, mesh=mesh, in_specs=in_specs, out_specs=out_specs, check_vma=False)
```

```python
import math

import jax
import jax.numpy as jnp
from jax import lax
from jax.sharding import Mesh
from jax.sharding import PartitionSpec as P

KRYLOV = 4


epsilon = 1e-06
time_step = 0.1
compress = 0.5
inflation = 4.0


CELL = ("cy", "cz")


def cell_sum(values):
    return lax.psum(lax.psum(values, "cz"), "cy")


def with_halo(block, sides, width):
    for axis, dim in sides:
        count = lax.axis_size(axis[0]) * lax.axis_size(axis[1])
        forward = [(i, i + 1) for i in range(count - 1)]
        backward = [(target, source) for source, target in forward]
        low = lax.ppermute(
            lax.slice_in_dim(block, block.shape[dim] - width, None, axis=dim), axis, forward
        )
        high = lax.ppermute(lax.slice_in_dim(block, 0, width, axis=dim), axis, backward)
        block = jnp.concatenate([low, block, high], axis=dim)
    return block


def mobility(sat_field):
    return sat_field * sat_field + 0.5 * (1.0 - sat_field) * (1.0 - sat_field)


def face_pair(perm_low, perm_high, sat_low, sat_high):
    trans = (
        2.0
        * perm_low
        * perm_high
        / (perm_low + perm_high)
        * (0.5 * (mobility(sat_low) + mobility(sat_high)))
    )
    return (trans, trans * (0.5 * (sat_low + sat_high)))


def plane_faces(perm, sat_field):
    plane_rows = perm.shape[-2]
    plane_cols = perm.shape[-1]
    keep_rows = (
        lax.broadcasted_iota(jnp.int32, (plane_rows, plane_cols), 0) < plane_rows - 1
    ).astype(jnp.float32)
    keep_cols = (
        lax.broadcasted_iota(jnp.int32, (plane_rows, plane_cols), 1) < plane_cols - 1
    ).astype(jnp.float32)
    trans_y, frac_y = face_pair(
        perm, jnp.roll(perm, -1, -2), sat_field, jnp.roll(sat_field, -1, -2)
    )
    trans_z, frac_z = face_pair(
        perm, jnp.roll(perm, -1, -1), sat_field, jnp.roll(sat_field, -1, -1)
    )
    return (trans_y * keep_rows, frac_y * keep_rows, trans_z * keep_cols, frac_z * keep_cols)


def operator(padded, second, coeffs):
    accum, trans_x, frac_x, trans_y, frac_y, trans_z, frac_z = coeffs
    first = padded[..., 1:-1, :, :]
    diff_x = padded[..., 1:, :, :] - padded[..., :-1, :, :]
    diff_y = jnp.roll(first, -1, -2) - first
    diff_z = jnp.roll(first, -1, -1) - first

    def net(coef_x, coef_y, coef_z):
        flow_x = coef_x * diff_x
        flow_y = coef_y * diff_y
        flow_z = coef_z * diff_z
        return (
            flow_x[..., :-1, :, :]
            - flow_x[..., 1:, :, :]
            + (jnp.roll(flow_y, 1, -2) - flow_y)
            + (jnp.roll(flow_z, 1, -1) - flow_z)
        )

    out_pressure = accum * (compress * first + 0.5 * second) + net(trans_x, trans_y, trans_z)
    out_water = accum * second + net(frac_x, frac_y, frac_z)
    return (out_pressure, out_water)


def least_squares(columns, beta):
    rows = [list(column) for column in columns]
    cosines = []
    sines = []
    target = [beta] + [jnp.zeros_like(beta) for column in columns]
    for jdx in range(len(rows)):
        column = rows[jdx]
        for idx in range(jdx):
            upper = cosines[idx] * column[idx] + sines[idx] * column[idx + 1]
            column[idx + 1] = -sines[idx] * column[idx] + cosines[idx] * column[idx + 1]
            column[idx] = upper
        radius = jnp.sqrt(column[jdx] * column[jdx] + column[jdx + 1] * column[jdx + 1])
        cosines.append(column[jdx] / radius)
        sines.append(column[jdx + 1] / radius)
        column[jdx] = radius
        target[jdx + 1] = -sines[jdx] * target[jdx]
        target[jdx] = cosines[jdx] * target[jdx]
    count = len(rows)
    solved = [None] * count
    for jdx in reversed(range(count)):
        partial_sum = target[jdx]
        for idx in range(jdx + 1, count):
            partial_sum = partial_sum - rows[idx][jdx] * solved[idx]
        solved[jdx] = partial_sum / rows[jdx][jdx]
    return solved


def ensemble_weights(predicted, obs_values, obs_error, noise):
    members = predicted.shape[0]
    sigma = math.sqrt(inflation) * obs_error
    center = jnp.mean(predicted, axis=0)
    spread = (predicted - center) / (math.sqrt(members - 1.0) * sigma)
    innov = (obs_values + sigma * noise - predicted) / sigma
    gram = jnp.eye(members, dtype=jnp.float32) + jnp.dot(
        spread, spread.T, precision=lax.Precision.HIGHEST, preferred_element_type=jnp.float32
    )
    cross = jnp.dot(
        spread, innov.T, precision=lax.Precision.HIGHEST, preferred_element_type=jnp.float32
    )
    factor = jnp.linalg.cholesky(gram)
    return jax.scipy.linalg.cho_solve((factor, True), cross)


def expand(values):
    return values[:, None, None, None, None]


def inner(left, right):
    return jnp.sum(left * right, axis=(1, 2, 3, 4))


def local(
    rhs, log_perm, porosity, saturation, pressure, obs_values, obs_error, noise, well_cell, obs_well
):
    local_members, slab_x, plane_rows, plane_cols = log_perm.shape
    members = noise.shape[0]
    plane = plane_rows * plane_cols
    cells_dev = slab_x * plane
    slab_index = lax.axis_index("cy") * lax.axis_size("cz") + lax.axis_index("cz")
    slab_count = lax.axis_size("cy") * lax.axis_size("cz")
    stacked = jnp.stack([log_perm, saturation], axis=1)
    rimmed = with_halo(stacked, ((CELL, 2),), 1)
    perm_pad = jnp.exp(rimmed[:, 0])
    sat_pad = rimmed[:, 1]
    trans_x, frac_x = face_pair(perm_pad[:, :-1], perm_pad[:, 1:], sat_pad[:, :-1], sat_pad[:, 1:])
    face_pos = lax.broadcasted_iota(jnp.int32, (slab_x + 1, 1, 1), 0)
    keep_face = jnp.where(
        face_pos == 0,
        slab_index > 0,
        jnp.where(face_pos == slab_x, slab_index < slab_count - 1, True),
    ).astype(jnp.float32)
    trans_x = trans_x * keep_face
    frac_x = frac_x * keep_face
    trans_y, frac_y, trans_z, frac_z = plane_faces(perm_pad[:, 1:-1], saturation)
    coeffs = (porosity / time_step, trans_x, frac_x, trans_y, frac_y, trans_z, frac_z)
    count = slab_count
    forward = [(i, i + 1) for i in range(count - 1)]
    backward = [(target, source) for source, target in forward]

    def planes(field):
        low = lax.ppermute(field[:, -1:], CELL, forward)
        high = lax.ppermute(field[:, :1], CELL, backward)
        return (low, high)

    def apply(vector, ghosts):
        padded = jnp.concatenate([ghosts[0], vector[:, 0], ghosts[1]], axis=1)
        out_pressure, out_water = operator(padded, vector[:, 1], coeffs)
        return jnp.stack([out_pressure, out_water], 1)

    def scale_planes(ghosts, scale):
        factor = scale[:, None, None, None]
        return (ghosts[0] / factor, ghosts[1] / factor)

    rhs_planes = planes(rhs[:, 0])
    image = apply(rhs, rhs_planes)
    image_planes = planes(image[:, 0])
    reduced = cell_sum(jnp.stack([inner(rhs, rhs), inner(rhs, image)], 0))
    beta = jnp.sqrt(reduced[0] + epsilon)
    basis = [rhs / expand(beta)]
    basis_planes = [scale_planes(rhs_planes, beta)]
    image = image / expand(beta)
    image_planes = scale_planes(image_planes, beta)
    projected = [reduced[1] / (beta * beta)]
    columns = []
    for jdx in range(KRYLOV):
        ortho = image
        ortho_low, ortho_high = image_planes
        for idx in range(jdx + 1):
            ortho = ortho - expand(projected[idx]) * basis[idx]
            factor = projected[idx][:, None, None, None]
            ortho_low = ortho_low - factor * basis_planes[idx][0]
            ortho_high = ortho_high - factor * basis_planes[idx][1]
        ortho_planes = (ortho_low, ortho_high)
        if jdx == KRYLOV - 1:
            height = jnp.sqrt(cell_sum(inner(ortho, ortho)) + epsilon)
            columns.append(projected + [height])
            break
        image = apply(ortho, ortho_planes)
        image_planes = planes(image[:, 0])
        parts = [inner(ortho, ortho)]
        parts += [inner(basis[idx], image) for idx in range(jdx + 1)]
        parts.append(inner(ortho, image))
        reduced = cell_sum(jnp.stack(parts, 0))
        height = jnp.sqrt(reduced[0] + epsilon)
        columns.append(projected + [height])
        basis.append(ortho / expand(height))
        basis_planes.append(scale_planes(ortho_planes, height))
        image = image / expand(height)
        image_planes = scale_planes(image_planes, height)
        projected = [reduced[1 + idx] / height for idx in range(jdx + 1)]
        projected.append(reduced[jdx + 2] / (height * height))
    solved = least_squares(columns, beta)
    increment = expand(solved[0]) * basis[0]
    for jdx in range(1, KRYLOV):
        increment = increment + expand(solved[jdx]) * basis[jdx]
    flat = jnp.stack([pressure + increment[:, 0], saturation + increment[:, 1]], 1).reshape(
        local_members, 2 * cells_dev
    )
    cells = jnp.take(well_cell, obs_well)
    wells = well_cell.shape[0]
    component = (jnp.arange(obs_well.shape[0], dtype=jnp.int32) >= wells).astype(jnp.int32)
    slab_row = cells // plane - slab_index * slab_x
    inside = (slab_row >= 0) & (slab_row < slab_x)
    local_cell = jnp.where(inside, slab_row * plane + cells % plane, 0)
    picked = jnp.take(flat, component * cells_dev + local_cell, axis=1) * inside.astype(jnp.float32)
    slab_pred = cell_sum(picked)
    predicted = lax.all_gather(slab_pred, "grp", axis=0, tiled=True)
    weights = ensemble_weights(predicted, obs_values, obs_error, noise)
    params = jnp.stack([log_perm, porosity], 1).reshape(local_members, 2 * cells_dev)
    offset = lax.axis_index("grp") * local_members
    scale_factor = 1.0 / math.sqrt(members - 1.0)
    scaled = params * scale_factor
    own_columns = lax.dynamic_slice_in_dim(weights, offset, local_members, 1)
    update = jnp.dot(
        own_columns.T,
        lax.all_gather(scaled, "grp", axis=0, tiled=True),
        precision=lax.Precision.HIGHEST,
        preferred_element_type=jnp.float32,
    )
    posterior = params + update
    posterior = posterior.reshape(local_members, 2, slab_x, plane_rows, plane_cols)
    return (increment, posterior[:, 0], posterior[:, 1])


def split_mesh(mesh):
    devices = mesh.devices
    groups, slabs = devices.shape
    along_z = len({device.coords[2] for device in devices[0]})
    return Mesh(devices.reshape(groups, slabs // along_z, along_z), ("grp", "cy", "cz"))


def solution(mesh):
    mesh = split_mesh(mesh)
    in_specs = (
        P("grp", None, CELL, None, None),
        P("grp", CELL, None, None),
        P("grp", CELL, None, None),
        P("grp", CELL, None, None),
        P("grp", CELL, None, None),
        P(),
        P(),
        P(),
        P(),
        P(),
    )
    out_specs = (
        P("grp", None, CELL, None, None),
        P("grp", CELL, None, None),
        P("grp", CELL, None, None),
    )
    return jax.shard_map(local, mesh=mesh, in_specs=in_specs, out_specs=out_specs, check_vma=False)
```

```python
import math

import jax
import jax.numpy as jnp
from jax import lax
from jax.sharding import Mesh
from jax.sharding import PartitionSpec as P

KRYLOV = 4


epsilon = 1e-06
time_step = 0.1
compress = 0.5
inflation = 4.0


CELL = ("cy", "cz")


def cell_sum(values, doubling=False):
    for axis in ("cz", "cy"):
        size = lax.axis_size(axis)
        if not doubling or size & (size - 1):
            values = lax.psum(values, axis)
            continue
        step = 1
        while step < size:
            values = values + lax.ppermute(values, axis, [(i, i ^ step) for i in range(size)])
            step *= 2
    return values


def with_halo(block, sides, width):
    for axis, dim in sides:
        count = lax.axis_size(axis[0]) * lax.axis_size(axis[1])
        forward = [(i, i + 1) for i in range(count - 1)]
        backward = [(target, source) for source, target in forward]
        low = lax.ppermute(
            lax.slice_in_dim(block, block.shape[dim] - width, None, axis=dim), axis, forward
        )
        high = lax.ppermute(lax.slice_in_dim(block, 0, width, axis=dim), axis, backward)
        block = jnp.concatenate([low, block, high], axis=dim)
    return block


def mobility(sat_field):
    return sat_field * sat_field + 0.5 * (1.0 - sat_field) * (1.0 - sat_field)


def face_pair(perm_low, perm_high, sat_low, sat_high):
    trans = (
        2.0
        * perm_low
        * perm_high
        / (perm_low + perm_high)
        * (0.5 * (mobility(sat_low) + mobility(sat_high)))
    )
    return (trans, trans * (0.5 * (sat_low + sat_high)))


def plane_faces(perm, sat_field):
    plane_rows = perm.shape[-2]
    plane_cols = perm.shape[-1]
    keep_rows = (
        lax.broadcasted_iota(jnp.int32, (plane_rows, plane_cols), 0) < plane_rows - 1
    ).astype(jnp.float32)
    keep_cols = (
        lax.broadcasted_iota(jnp.int32, (plane_rows, plane_cols), 1) < plane_cols - 1
    ).astype(jnp.float32)
    trans_y, frac_y = face_pair(
        perm, jnp.roll(perm, -1, -2), sat_field, jnp.roll(sat_field, -1, -2)
    )
    trans_z, frac_z = face_pair(
        perm, jnp.roll(perm, -1, -1), sat_field, jnp.roll(sat_field, -1, -1)
    )
    return (trans_y * keep_rows, frac_y * keep_rows, trans_z * keep_cols, frac_z * keep_cols)


def operator(padded, second, coeffs):
    accum, trans_x, frac_x, trans_y, frac_y, trans_z, frac_z = coeffs
    first = padded[..., 1:-1, :, :]
    diff_x = padded[..., 1:, :, :] - padded[..., :-1, :, :]
    diff_y = jnp.roll(first, -1, -2) - first
    diff_z = jnp.roll(first, -1, -1) - first

    def net(coef_x, coef_y, coef_z):
        flow_x = coef_x * diff_x
        flow_y = coef_y * diff_y
        flow_z = coef_z * diff_z
        return (
            flow_x[..., :-1, :, :]
            - flow_x[..., 1:, :, :]
            + (jnp.roll(flow_y, 1, -2) - flow_y)
            + (jnp.roll(flow_z, 1, -1) - flow_z)
        )

    out_pressure = accum * (compress * first + 0.5 * second) + net(trans_x, trans_y, trans_z)
    out_water = accum * second + net(frac_x, frac_y, frac_z)
    return (out_pressure, out_water)


def least_squares(columns, beta):
    rows = [list(column) for column in columns]
    cosines = []
    sines = []
    target = [beta] + [jnp.zeros_like(beta) for column in columns]
    for jdx in range(len(rows)):
        column = rows[jdx]
        for idx in range(jdx):
            upper = cosines[idx] * column[idx] + sines[idx] * column[idx + 1]
            column[idx + 1] = -sines[idx] * column[idx] + cosines[idx] * column[idx + 1]
            column[idx] = upper
        radius = jnp.sqrt(column[jdx] * column[jdx] + column[jdx + 1] * column[jdx + 1])
        cosines.append(column[jdx] / radius)
        sines.append(column[jdx + 1] / radius)
        column[jdx] = radius
        target[jdx + 1] = -sines[jdx] * target[jdx]
        target[jdx] = cosines[jdx] * target[jdx]
    count = len(rows)
    solved = [None] * count
    for jdx in reversed(range(count)):
        partial_sum = target[jdx]
        for idx in range(jdx + 1, count):
            partial_sum = partial_sum - rows[idx][jdx] * solved[idx]
        solved[jdx] = partial_sum / rows[jdx][jdx]
    return solved


def ensemble_weights(predicted, obs_values, obs_error, noise):
    members = predicted.shape[0]
    sigma = math.sqrt(inflation) * obs_error
    center = jnp.mean(predicted, axis=0)
    spread = (predicted - center) / (math.sqrt(members - 1.0) * sigma)
    innov = (obs_values + sigma * noise - predicted) / sigma
    gram = jnp.eye(members, dtype=jnp.float32) + jnp.dot(
        spread, spread.T, precision=lax.Precision.HIGHEST, preferred_element_type=jnp.float32
    )
    cross = jnp.dot(
        spread, innov.T, precision=lax.Precision.HIGHEST, preferred_element_type=jnp.float32
    )
    factor = jnp.linalg.cholesky(gram)
    return jax.scipy.linalg.cho_solve((factor, True), cross)


def expand(values):
    return values[:, None, None, None, None]


def inner(left, right):
    return jnp.sum(left * right, axis=(1, 2, 3, 4))


def local(
    rhs, log_perm, porosity, saturation, pressure, obs_values, obs_error, noise, well_cell, obs_well
):
    local_members, slab_x, plane_rows, plane_cols = log_perm.shape
    members = noise.shape[0]
    plane = plane_rows * plane_cols
    cells_dev = slab_x * plane
    slab_index = lax.axis_index("cy") * lax.axis_size("cz") + lax.axis_index("cz")
    slab_count = lax.axis_size("cy") * lax.axis_size("cz")
    stacked = jnp.stack([log_perm, saturation], axis=1)
    rimmed = with_halo(stacked, ((CELL, 2),), 1)
    perm_pad = jnp.exp(rimmed[:, 0])
    sat_pad = rimmed[:, 1]
    trans_x, frac_x = face_pair(perm_pad[:, :-1], perm_pad[:, 1:], sat_pad[:, :-1], sat_pad[:, 1:])
    face_pos = lax.broadcasted_iota(jnp.int32, (slab_x + 1, 1, 1), 0)
    keep_face = jnp.where(
        face_pos == 0,
        slab_index > 0,
        jnp.where(face_pos == slab_x, slab_index < slab_count - 1, True),
    ).astype(jnp.float32)
    trans_x = trans_x * keep_face
    frac_x = frac_x * keep_face
    trans_y, frac_y, trans_z, frac_z = plane_faces(perm_pad[:, 1:-1], saturation)
    coeffs = (porosity / time_step, trans_x, frac_x, trans_y, frac_y, trans_z, frac_z)
    count = slab_count
    forward = [(i, i + 1) for i in range(count - 1)]
    backward = [(target, source) for source, target in forward]

    def planes(field):
        low = lax.ppermute(field[:, -1:], CELL, forward)
        high = lax.ppermute(field[:, :1], CELL, backward)
        return (low, high)

    def apply(vector, ghosts):
        padded = jnp.concatenate([ghosts[0], vector[:, 0], ghosts[1]], axis=1)
        out_pressure, out_water = operator(padded, vector[:, 1], coeffs)
        return jnp.stack([out_pressure, out_water], 1)

    def scale_planes(ghosts, scale):
        factor = scale[:, None, None, None]
        return (ghosts[0] / factor, ghosts[1] / factor)

    rhs_planes = planes(rhs[:, 0])
    image = apply(rhs, rhs_planes)
    image_planes = planes(image[:, 0])
    reduced = cell_sum(jnp.stack([inner(rhs, rhs), inner(rhs, image)], 0))
    beta = jnp.sqrt(reduced[0] + epsilon)
    basis = [rhs / expand(beta)]
    basis_planes = [scale_planes(rhs_planes, beta)]
    image = image / expand(beta)
    image_planes = scale_planes(image_planes, beta)
    projected = [reduced[1] / (beta * beta)]
    columns = []
    for jdx in range(KRYLOV):
        ortho = image
        ortho_low, ortho_high = image_planes
        for idx in range(jdx + 1):
            ortho = ortho - expand(projected[idx]) * basis[idx]
            factor = projected[idx][:, None, None, None]
            ortho_low = ortho_low - factor * basis_planes[idx][0]
            ortho_high = ortho_high - factor * basis_planes[idx][1]
        ortho_planes = (ortho_low, ortho_high)
        if jdx == KRYLOV - 1:
            height = jnp.sqrt(cell_sum(inner(ortho, ortho)) + epsilon)
            columns.append(projected + [height])
            break
        image = apply(ortho, ortho_planes)
        image_planes = planes(image[:, 0])
        parts = [inner(ortho, ortho)]
        parts += [inner(basis[idx], image) for idx in range(jdx + 1)]
        parts.append(inner(ortho, image))
        reduced = cell_sum(jnp.stack(parts, 0))
        height = jnp.sqrt(reduced[0] + epsilon)
        columns.append(projected + [height])
        basis.append(ortho / expand(height))
        basis_planes.append(scale_planes(ortho_planes, height))
        image = image / expand(height)
        image_planes = scale_planes(image_planes, height)
        projected = [reduced[1 + idx] / height for idx in range(jdx + 1)]
        projected.append(reduced[jdx + 2] / (height * height))
    solved = least_squares(columns, beta)
    increment = expand(solved[0]) * basis[0]
    for jdx in range(1, KRYLOV):
        increment = increment + expand(solved[jdx]) * basis[jdx]
    cells = jnp.take(well_cell, obs_well)
    wells = well_cell.shape[0]
    component = (jnp.arange(obs_well.shape[0], dtype=jnp.int32) >= wells).astype(jnp.int32)
    slab_row = cells // plane - slab_index * slab_x
    inside = (slab_row >= 0) & (slab_row < slab_x)
    row = jnp.where(inside, slab_row, 0)
    col_y = (cells % plane) // plane_cols
    col_z = cells % plane_cols
    state = jnp.where(
        component[None, :] > 0,
        saturation[:, row, col_y, col_z],
        pressure[:, row, col_y, col_z],
    )
    picked = (state + increment[:, component, row, col_y, col_z]) * inside.astype(jnp.float32)
    slab_pred = cell_sum(picked, doubling=True)
    predicted = lax.all_gather(slab_pred, "grp", axis=0, tiled=True)
    weights = ensemble_weights(predicted, obs_values, obs_error, noise)
    params = jnp.stack([log_perm, porosity], 1).reshape(local_members, 2 * cells_dev)
    offset = lax.axis_index("grp") * local_members
    scale_factor = 1.0 / math.sqrt(members - 1.0)
    scaled = params * scale_factor
    own_columns = lax.dynamic_slice_in_dim(weights, offset, local_members, 1)
    update = jnp.dot(
        own_columns.T,
        lax.all_gather(scaled, "grp", axis=0, tiled=True),
        precision=lax.Precision.HIGHEST,
        preferred_element_type=jnp.float32,
    )
    posterior = params + update
    posterior = posterior.reshape(local_members, 2, slab_x, plane_rows, plane_cols)
    return (increment, posterior[:, 0], posterior[:, 1])


def split_mesh(mesh):
    devices = mesh.devices
    groups, slabs = devices.shape
    along_z = len({device.coords[2] for device in devices[0]})
    return Mesh(devices.reshape(groups, slabs // along_z, along_z), ("grp", "cy", "cz"))


def solution(mesh):
    mesh = split_mesh(mesh)
    in_specs = (
        P("grp", None, CELL, None, None),
        P("grp", CELL, None, None),
        P("grp", CELL, None, None),
        P("grp", CELL, None, None),
        P("grp", CELL, None, None),
        P(),
        P(),
        P(),
        P(),
        P(),
    )
    out_specs = (
        P("grp", None, CELL, None, None),
        P("grp", CELL, None, None),
        P("grp", CELL, None, None),
    )
    return jax.shard_map(local, mesh=mesh, in_specs=in_specs, out_specs=out_specs, check_vma=False)
```

```python
import math

import jax
import jax.numpy as jnp
from jax import lax
from jax.sharding import Mesh
from jax.sharding import PartitionSpec as P

KRYLOV = 4


epsilon = 1e-06
time_step = 0.1
compress = 0.5
inflation = 4.0


CELL = ("cy", "cz")


def cell_sum(values, doubling=False):
    for axis in ("cz", "cy"):
        size = lax.axis_size(axis)
        if not doubling or size & (size - 1):
            values = lax.psum(values, axis)
            continue
        step = 1
        while step < size:
            values = values + lax.ppermute(values, axis, [(i, i ^ step) for i in range(size)])
            step *= 2
    return values


def with_halo(block, sides, width):
    for axis, dim in sides:
        count = lax.axis_size(axis[0]) * lax.axis_size(axis[1])
        forward = [(i, i + 1) for i in range(count - 1)]
        backward = [(target, source) for source, target in forward]
        low = lax.ppermute(
            lax.slice_in_dim(block, block.shape[dim] - width, None, axis=dim), axis, forward
        )
        high = lax.ppermute(lax.slice_in_dim(block, 0, width, axis=dim), axis, backward)
        block = jnp.concatenate([low, block, high], axis=dim)
    return block


def mobility(sat_field):
    return sat_field * sat_field + 0.5 * (1.0 - sat_field) * (1.0 - sat_field)


def face_pair(perm_low, perm_high, sat_low, sat_high):
    trans = (
        2.0
        * perm_low
        * perm_high
        / (perm_low + perm_high)
        * (0.5 * (mobility(sat_low) + mobility(sat_high)))
    )
    return (trans, trans * (0.5 * (sat_low + sat_high)))


def plane_faces(perm, sat_field):
    plane_rows = perm.shape[-2]
    plane_cols = perm.shape[-1]
    keep_rows = (
        lax.broadcasted_iota(jnp.int32, (plane_rows, plane_cols), 0) < plane_rows - 1
    ).astype(jnp.float32)
    keep_cols = (
        lax.broadcasted_iota(jnp.int32, (plane_rows, plane_cols), 1) < plane_cols - 1
    ).astype(jnp.float32)
    trans_y, frac_y = face_pair(
        perm, jnp.roll(perm, -1, -2), sat_field, jnp.roll(sat_field, -1, -2)
    )
    trans_z, frac_z = face_pair(
        perm, jnp.roll(perm, -1, -1), sat_field, jnp.roll(sat_field, -1, -1)
    )
    return (trans_y * keep_rows, frac_y * keep_rows, trans_z * keep_cols, frac_z * keep_cols)


def operator(padded, second, coeffs):
    accum, trans_x, frac_x, trans_y, frac_y, trans_z, frac_z = coeffs
    first = padded[..., 1:-1, :, :]
    diff_x = padded[..., 1:, :, :] - padded[..., :-1, :, :]
    diff_y = jnp.roll(first, -1, -2) - first
    diff_z = jnp.roll(first, -1, -1) - first

    def net(coef_x, coef_y, coef_z):
        flow_x = coef_x * diff_x
        flow_y = coef_y * diff_y
        flow_z = coef_z * diff_z
        return (
            flow_x[..., :-1, :, :]
            - flow_x[..., 1:, :, :]
            + (jnp.roll(flow_y, 1, -2) - flow_y)
            + (jnp.roll(flow_z, 1, -1) - flow_z)
        )

    out_pressure = accum * (compress * first + 0.5 * second) + net(trans_x, trans_y, trans_z)
    out_water = accum * second + net(frac_x, frac_y, frac_z)
    return (out_pressure, out_water)


def least_squares(columns, beta):
    rows = [list(column) for column in columns]
    cosines = []
    sines = []
    target = [beta] + [jnp.zeros_like(beta) for column in columns]
    for jdx in range(len(rows)):
        column = rows[jdx]
        for idx in range(jdx):
            upper = cosines[idx] * column[idx] + sines[idx] * column[idx + 1]
            column[idx + 1] = -sines[idx] * column[idx] + cosines[idx] * column[idx + 1]
            column[idx] = upper
        radius = jnp.sqrt(column[jdx] * column[jdx] + column[jdx + 1] * column[jdx + 1])
        cosines.append(column[jdx] / radius)
        sines.append(column[jdx + 1] / radius)
        column[jdx] = radius
        target[jdx + 1] = -sines[jdx] * target[jdx]
        target[jdx] = cosines[jdx] * target[jdx]
    count = len(rows)
    solved = [None] * count
    for jdx in reversed(range(count)):
        partial_sum = target[jdx]
        for idx in range(jdx + 1, count):
            partial_sum = partial_sum - rows[idx][jdx] * solved[idx]
        solved[jdx] = partial_sum / rows[jdx][jdx]
    return solved


def ensemble_weights(predicted, obs_values, obs_error, noise, offset, count):
    members = predicted.shape[0]
    sigma = math.sqrt(inflation) * obs_error
    center = jnp.mean(predicted, axis=0)
    spread = (predicted - center) / (math.sqrt(members - 1.0) * sigma)
    innov = (obs_values + sigma * noise - predicted) / sigma
    own_innov = lax.dynamic_slice_in_dim(innov, offset, count, 0)
    gram = jnp.eye(members, dtype=jnp.float32) + jnp.dot(
        spread, spread.T, precision=lax.Precision.HIGHEST, preferred_element_type=jnp.float32
    )
    cross = jnp.dot(
        spread, own_innov.T, precision=lax.Precision.HIGHEST, preferred_element_type=jnp.float32
    )
    factor = jnp.linalg.cholesky(gram)
    return jax.scipy.linalg.cho_solve((factor, True), cross)


def expand(values):
    return values[:, None, None, None, None]


def inner(left, right):
    return jnp.sum(left * right, axis=(1, 2, 3, 4))


def local(
    rhs, log_perm, porosity, saturation, pressure, obs_values, obs_error, noise, well_cell, obs_well
):
    local_members, slab_x, plane_rows, plane_cols = log_perm.shape
    members = noise.shape[0]
    plane = plane_rows * plane_cols
    cells_dev = slab_x * plane
    slab_index = lax.axis_index("cy") * lax.axis_size("cz") + lax.axis_index("cz")
    slab_count = lax.axis_size("cy") * lax.axis_size("cz")
    stacked = jnp.stack([log_perm, saturation], axis=1)
    rimmed = with_halo(stacked, ((CELL, 2),), 1)
    perm_pad = jnp.exp(rimmed[:, 0])
    sat_pad = rimmed[:, 1]
    trans_x, frac_x = face_pair(perm_pad[:, :-1], perm_pad[:, 1:], sat_pad[:, :-1], sat_pad[:, 1:])
    face_pos = lax.broadcasted_iota(jnp.int32, (slab_x + 1, 1, 1), 0)
    keep_face = jnp.where(
        face_pos == 0,
        slab_index > 0,
        jnp.where(face_pos == slab_x, slab_index < slab_count - 1, True),
    ).astype(jnp.float32)
    trans_x = trans_x * keep_face
    frac_x = frac_x * keep_face
    trans_y, frac_y, trans_z, frac_z = plane_faces(perm_pad[:, 1:-1], saturation)
    coeffs = (porosity / time_step, trans_x, frac_x, trans_y, frac_y, trans_z, frac_z)
    count = slab_count
    forward = [(i, i + 1) for i in range(count - 1)]
    backward = [(target, source) for source, target in forward]

    def planes(field):
        low = lax.ppermute(field[:, -1:], CELL, forward)
        high = lax.ppermute(field[:, :1], CELL, backward)
        return (low, high)

    def apply(vector, ghosts):
        padded = jnp.concatenate([ghosts[0], vector[:, 0], ghosts[1]], axis=1)
        out_pressure, out_water = operator(padded, vector[:, 1], coeffs)
        return jnp.stack([out_pressure, out_water], 1)

    def scale_planes(ghosts, scale):
        factor = scale[:, None, None, None]
        return (ghosts[0] / factor, ghosts[1] / factor)

    rhs_planes = planes(rhs[:, 0])
    image = apply(rhs, rhs_planes)
    image_planes = planes(image[:, 0])
    reduced = cell_sum(jnp.stack([inner(rhs, rhs), inner(rhs, image)], 0))
    beta = jnp.sqrt(reduced[0] + epsilon)
    basis = [rhs / expand(beta)]
    basis_planes = [scale_planes(rhs_planes, beta)]
    image = image / expand(beta)
    image_planes = scale_planes(image_planes, beta)
    projected = [reduced[1] / (beta * beta)]
    columns = []
    for jdx in range(KRYLOV):
        ortho = image
        ortho_low, ortho_high = image_planes
        for idx in range(jdx + 1):
            ortho = ortho - expand(projected[idx]) * basis[idx]
            factor = projected[idx][:, None, None, None]
            ortho_low = ortho_low - factor * basis_planes[idx][0]
            ortho_high = ortho_high - factor * basis_planes[idx][1]
        ortho_planes = (ortho_low, ortho_high)
        if jdx == KRYLOV - 1:
            height = jnp.sqrt(cell_sum(inner(ortho, ortho)) + epsilon)
            columns.append(projected + [height])
            break
        image = apply(ortho, ortho_planes)
        image_planes = planes(image[:, 0])
        parts = [inner(ortho, ortho)]
        parts += [inner(basis[idx], image) for idx in range(jdx + 1)]
        parts.append(inner(ortho, image))
        reduced = cell_sum(jnp.stack(parts, 0))
        height = jnp.sqrt(reduced[0] + epsilon)
        columns.append(projected + [height])
        basis.append(ortho / expand(height))
        basis_planes.append(scale_planes(ortho_planes, height))
        image = image / expand(height)
        image_planes = scale_planes(image_planes, height)
        projected = [reduced[1 + idx] / height for idx in range(jdx + 1)]
        projected.append(reduced[jdx + 2] / (height * height))
    solved = least_squares(columns, beta)
    increment = expand(solved[0]) * basis[0]
    for jdx in range(1, KRYLOV):
        increment = increment + expand(solved[jdx]) * basis[jdx]
    cells = jnp.take(well_cell, obs_well)
    wells = well_cell.shape[0]
    component = (jnp.arange(obs_well.shape[0], dtype=jnp.int32) >= wells).astype(jnp.int32)
    slab_row = cells // plane - slab_index * slab_x
    inside = (slab_row >= 0) & (slab_row < slab_x)
    rows = 2 * slab_x * plane_rows
    row = component * (slab_x * plane_rows) + slab_row * plane_rows + (cells % plane) // plane_cols
    col_z = cells % plane_cols
    state = jnp.stack([pressure + increment[:, 0], saturation + increment[:, 1]], 1)
    table = state.reshape(local_members * rows, plane_cols)
    pick_z = (lax.broadcasted_iota(jnp.int32, (plane_cols, cells.shape[0]), 0) == col_z[None, :])
    by_row = jnp.dot(
        table,
        pick_z.astype(jnp.float32),
        precision=lax.Precision.HIGHEST,
        preferred_element_type=jnp.float32,
    )
    pick_row = (lax.broadcasted_iota(jnp.int32, (rows, cells.shape[0]), 0) == row[None, :]) & inside[None, :]
    picked = jnp.sum(
        by_row.reshape(local_members, rows, cells.shape[0]) * pick_row.astype(jnp.float32)[None],
        axis=1,
    )
    slab_pred = cell_sum(picked, doubling=True)
    predicted = lax.all_gather(slab_pred, "grp", axis=0, tiled=True)
    params = jnp.stack([log_perm, porosity], 1).reshape(local_members, 2 * cells_dev)
    offset = lax.axis_index("grp") * local_members
    own_columns = ensemble_weights(predicted, obs_values, obs_error, noise, offset, local_members)
    scale_factor = 1.0 / math.sqrt(members - 1.0)
    scaled = params * scale_factor
    update = jnp.dot(
        own_columns.T,
        lax.all_gather(scaled, "grp", axis=0, tiled=True),
        precision=lax.Precision.HIGHEST,
        preferred_element_type=jnp.float32,
    )
    posterior = params + update
    posterior = posterior.reshape(local_members, 2, slab_x, plane_rows, plane_cols)
    return (increment, posterior[:, 0], posterior[:, 1])


def split_mesh(mesh):
    devices = mesh.devices
    groups, slabs = devices.shape
    along_z = len({device.coords[2] for device in devices[0]})
    return Mesh(devices.reshape(groups, slabs // along_z, along_z), ("grp", "cy", "cz"))


def solution(mesh):
    mesh = split_mesh(mesh)
    in_specs = (
        P("grp", None, CELL, None, None),
        P("grp", CELL, None, None),
        P("grp", CELL, None, None),
        P("grp", CELL, None, None),
        P("grp", CELL, None, None),
        P(),
        P(),
        P(),
        P(),
        P(),
    )
    out_specs = (
        P("grp", None, CELL, None, None),
        P("grp", CELL, None, None),
        P("grp", CELL, None, None),
    )
    return jax.shard_map(local, mesh=mesh, in_specs=in_specs, out_specs=out_specs, check_vma=False)
```

```python
import math

import jax
import jax.numpy as jnp
from jax import lax
from jax.sharding import Mesh
from jax.sharding import PartitionSpec as P

KRYLOV = 4


epsilon = 1e-06
time_step = 0.1
compress = 0.5
inflation = 4.0


CELL = ("cy", "cz")


def cell_sum(values, doubling=False):
    for axis in ("cz", "cy"):
        size = lax.axis_size(axis)
        if not doubling or size & (size - 1):
            values = lax.psum(values, axis)
            continue
        step = 1
        while step < size:
            values = values + lax.ppermute(values, axis, [(i, i ^ step) for i in range(size)])
            step *= 2
    return values


def with_halo(block, sides, width):
    for axis, dim in sides:
        count = lax.axis_size(axis[0]) * lax.axis_size(axis[1])
        forward = [(i, i + 1) for i in range(count - 1)]
        backward = [(target, source) for source, target in forward]
        low = lax.ppermute(
            lax.slice_in_dim(block, block.shape[dim] - width, None, axis=dim), axis, forward
        )
        high = lax.ppermute(lax.slice_in_dim(block, 0, width, axis=dim), axis, backward)
        block = jnp.concatenate([low, block, high], axis=dim)
    return block


def mobility(sat_field):
    return sat_field * sat_field + 0.5 * (1.0 - sat_field) * (1.0 - sat_field)


def face_pair(perm_low, perm_high, sat_low, sat_high):
    trans = (
        2.0
        * perm_low
        * perm_high
        / (perm_low + perm_high)
        * (0.5 * (mobility(sat_low) + mobility(sat_high)))
    )
    return (trans, trans * (0.5 * (sat_low + sat_high)))


def plane_faces(perm, sat_field):
    plane_rows = perm.shape[-2]
    plane_cols = perm.shape[-1]
    keep_rows = (
        lax.broadcasted_iota(jnp.int32, (plane_rows, plane_cols), 0) < plane_rows - 1
    ).astype(jnp.float32)
    keep_cols = (
        lax.broadcasted_iota(jnp.int32, (plane_rows, plane_cols), 1) < plane_cols - 1
    ).astype(jnp.float32)
    trans_y, frac_y = face_pair(
        perm, jnp.roll(perm, -1, -2), sat_field, jnp.roll(sat_field, -1, -2)
    )
    trans_z, frac_z = face_pair(
        perm, jnp.roll(perm, -1, -1), sat_field, jnp.roll(sat_field, -1, -1)
    )
    return (trans_y * keep_rows, frac_y * keep_rows, trans_z * keep_cols, frac_z * keep_cols)


def operator(padded, second, coeffs):
    accum, trans_x, frac_x, trans_y, frac_y, trans_z, frac_z = coeffs
    first = padded[..., 1:-1, :, :]
    diff_x = padded[..., 1:, :, :] - padded[..., :-1, :, :]
    diff_y = jnp.roll(first, -1, -2) - first
    diff_z = jnp.roll(first, -1, -1) - first

    def net(coef_x, coef_y, coef_z):
        flow_x = coef_x * diff_x
        flow_y = coef_y * diff_y
        flow_z = coef_z * diff_z
        return (
            flow_x[..., :-1, :, :]
            - flow_x[..., 1:, :, :]
            + (jnp.roll(flow_y, 1, -2) - flow_y)
            + (jnp.roll(flow_z, 1, -1) - flow_z)
        )

    out_pressure = accum * (compress * first + 0.5 * second) + net(trans_x, trans_y, trans_z)
    out_water = accum * second + net(frac_x, frac_y, frac_z)
    return (out_pressure, out_water)


def least_squares(columns, beta):
    rows = [list(column) for column in columns]
    cosines = []
    sines = []
    target = [beta] + [jnp.zeros_like(beta) for column in columns]
    for jdx in range(len(rows)):
        column = rows[jdx]
        for idx in range(jdx):
            upper = cosines[idx] * column[idx] + sines[idx] * column[idx + 1]
            column[idx + 1] = -sines[idx] * column[idx] + cosines[idx] * column[idx + 1]
            column[idx] = upper
        radius = jnp.sqrt(column[jdx] * column[jdx] + column[jdx + 1] * column[jdx + 1])
        cosines.append(column[jdx] / radius)
        sines.append(column[jdx + 1] / radius)
        column[jdx] = radius
        target[jdx + 1] = -sines[jdx] * target[jdx]
        target[jdx] = cosines[jdx] * target[jdx]
    count = len(rows)
    solved = [None] * count
    for jdx in reversed(range(count)):
        partial_sum = target[jdx]
        for idx in range(jdx + 1, count):
            partial_sum = partial_sum - rows[idx][jdx] * solved[idx]
        solved[jdx] = partial_sum / rows[jdx][jdx]
    return solved


def ensemble_weights(predicted, obs_values, obs_error, noise, offset, count):
    members = predicted.shape[0]
    sigma = math.sqrt(inflation) * obs_error
    center = jnp.mean(predicted, axis=0)
    spread = (predicted - center) / (math.sqrt(members - 1.0) * sigma)
    innov = (obs_values + sigma * noise - predicted) / sigma
    own_innov = lax.dynamic_slice_in_dim(innov, offset, count, 0)
    gram = jnp.eye(members, dtype=jnp.float32) + jnp.dot(
        spread, spread.T, precision=lax.Precision.HIGHEST, preferred_element_type=jnp.float32
    )
    cross = jnp.dot(
        spread, own_innov.T, precision=lax.Precision.HIGHEST, preferred_element_type=jnp.float32
    )
    factor = jnp.linalg.cholesky(gram)
    return jax.scipy.linalg.cho_solve((factor, True), cross)


def expand(values):
    return values[:, None, None, None, None]


def inner(left, right):
    return jnp.sum(left * right, axis=(1, 2, 3, 4))


def local(
    rhs, log_perm, porosity, saturation, pressure, obs_values, obs_error, noise, well_cell, obs_well
):
    local_members, slab_x, plane_rows, plane_cols = log_perm.shape
    members = noise.shape[0]
    plane = plane_rows * plane_cols
    cells_dev = slab_x * plane
    slab_index = lax.axis_index("cy") * lax.axis_size("cz") + lax.axis_index("cz")
    slab_count = lax.axis_size("cy") * lax.axis_size("cz")
    count = slab_count
    forward = [(i, i + 1) for i in range(count - 1)]
    backward = [(target, source) for source, target in forward]
    edges = (log_perm, saturation, rhs[:, 0])
    low = lax.ppermute(jnp.stack([field[:, -1:] for field in edges], 1), CELL, forward)
    high = lax.ppermute(jnp.stack([field[:, :1] for field in edges], 1), CELL, backward)
    perm_pad = jnp.exp(jnp.concatenate([low[:, 0], log_perm, high[:, 0]], axis=1))
    sat_pad = jnp.concatenate([low[:, 1], saturation, high[:, 1]], axis=1)
    trans_x, frac_x = face_pair(perm_pad[:, :-1], perm_pad[:, 1:], sat_pad[:, :-1], sat_pad[:, 1:])
    face_pos = lax.broadcasted_iota(jnp.int32, (slab_x + 1, 1, 1), 0)
    keep_face = jnp.where(
        face_pos == 0,
        slab_index > 0,
        jnp.where(face_pos == slab_x, slab_index < slab_count - 1, True),
    ).astype(jnp.float32)
    trans_x = trans_x * keep_face
    frac_x = frac_x * keep_face
    trans_y, frac_y, trans_z, frac_z = plane_faces(perm_pad[:, 1:-1], saturation)
    coeffs = (porosity / time_step, trans_x, frac_x, trans_y, frac_y, trans_z, frac_z)

    def planes(field):
        low = lax.ppermute(field[:, -1:], CELL, forward)
        high = lax.ppermute(field[:, :1], CELL, backward)
        return (low, high)

    def apply(vector, ghosts):
        padded = jnp.concatenate([ghosts[0], vector[:, 0], ghosts[1]], axis=1)
        out_pressure, out_water = operator(padded, vector[:, 1], coeffs)
        return jnp.stack([out_pressure, out_water], 1)

    def scale_planes(ghosts, scale):
        factor = scale[:, None, None, None]
        return (ghosts[0] / factor, ghosts[1] / factor)

    rhs_planes = (low[:, 2], high[:, 2])
    image = apply(rhs, rhs_planes)
    image_planes = planes(image[:, 0])
    reduced = cell_sum(jnp.stack([inner(rhs, rhs), inner(rhs, image)], 0))
    beta = jnp.sqrt(reduced[0] + epsilon)
    basis = [rhs / expand(beta)]
    basis_planes = [scale_planes(rhs_planes, beta)]
    image = image / expand(beta)
    image_planes = scale_planes(image_planes, beta)
    projected = [reduced[1] / (beta * beta)]
    columns = []
    for jdx in range(KRYLOV):
        ortho = image
        ortho_low, ortho_high = image_planes
        for idx in range(jdx + 1):
            ortho = ortho - expand(projected[idx]) * basis[idx]
            factor = projected[idx][:, None, None, None]
            ortho_low = ortho_low - factor * basis_planes[idx][0]
            ortho_high = ortho_high - factor * basis_planes[idx][1]
        ortho_planes = (ortho_low, ortho_high)
        if jdx == KRYLOV - 1:
            height = jnp.sqrt(cell_sum(inner(ortho, ortho)) + epsilon)
            columns.append(projected + [height])
            break
        image = apply(ortho, ortho_planes)
        image_planes = planes(image[:, 0])
        parts = [inner(ortho, ortho)]
        parts += [inner(basis[idx], image) for idx in range(jdx + 1)]
        parts.append(inner(ortho, image))
        reduced = cell_sum(jnp.stack(parts, 0))
        height = jnp.sqrt(reduced[0] + epsilon)
        columns.append(projected + [height])
        basis.append(ortho / expand(height))
        basis_planes.append(scale_planes(ortho_planes, height))
        image = image / expand(height)
        image_planes = scale_planes(image_planes, height)
        projected = [reduced[1 + idx] / height for idx in range(jdx + 1)]
        projected.append(reduced[jdx + 2] / (height * height))
    solved = least_squares(columns, beta)
    increment = expand(solved[0]) * basis[0]
    for jdx in range(1, KRYLOV):
        increment = increment + expand(solved[jdx]) * basis[jdx]
    cells = jnp.take(well_cell, obs_well)
    wells = well_cell.shape[0]
    component = (jnp.arange(obs_well.shape[0], dtype=jnp.int32) >= wells).astype(jnp.int32)
    slab_row = cells // plane - slab_index * slab_x
    inside = (slab_row >= 0) & (slab_row < slab_x)
    rows = 2 * slab_x * plane_rows
    row = component * (slab_x * plane_rows) + slab_row * plane_rows + (cells % plane) // plane_cols
    col_z = cells % plane_cols
    state = jnp.stack([pressure + increment[:, 0], saturation + increment[:, 1]], 1)
    table = state.reshape(local_members * rows, plane_cols)
    pick_z = (lax.broadcasted_iota(jnp.int32, (plane_cols, cells.shape[0]), 0) == col_z[None, :])
    by_row = jnp.dot(
        table,
        pick_z.astype(jnp.float32),
        precision=lax.Precision.HIGHEST,
        preferred_element_type=jnp.float32,
    )
    pick_row = (lax.broadcasted_iota(jnp.int32, (rows, cells.shape[0]), 0) == row[None, :]) & inside[None, :]
    picked = jnp.sum(
        by_row.reshape(local_members, rows, cells.shape[0]) * pick_row.astype(jnp.float32)[None],
        axis=1,
    )
    slab_pred = cell_sum(picked, doubling=True)
    predicted = lax.all_gather(slab_pred, "grp", axis=0, tiled=True)
    params = jnp.stack([log_perm, porosity], 1).reshape(local_members, 2 * cells_dev)
    offset = lax.axis_index("grp") * local_members
    own_columns = ensemble_weights(predicted, obs_values, obs_error, noise, offset, local_members)
    scale_factor = 1.0 / math.sqrt(members - 1.0)
    scaled = params * scale_factor
    update = jnp.dot(
        own_columns.T,
        lax.all_gather(scaled, "grp", axis=0, tiled=True),
        precision=lax.Precision.HIGHEST,
        preferred_element_type=jnp.float32,
    )
    posterior = params + update
    posterior = posterior.reshape(local_members, 2, slab_x, plane_rows, plane_cols)
    return (increment, posterior[:, 0], posterior[:, 1])


def split_mesh(mesh):
    devices = mesh.devices
    groups, slabs = devices.shape
    along_z = len({device.coords[2] for device in devices[0]})
    return Mesh(devices.reshape(groups, slabs // along_z, along_z), ("grp", "cy", "cz"))


def solution(mesh):
    mesh = split_mesh(mesh)
    in_specs = (
        P("grp", None, CELL, None, None),
        P("grp", CELL, None, None),
        P("grp", CELL, None, None),
        P("grp", CELL, None, None),
        P("grp", CELL, None, None),
        P(),
        P(),
        P(),
        P(),
        P(),
    )
    out_specs = (
        P("grp", None, CELL, None, None),
        P("grp", CELL, None, None),
        P("grp", CELL, None, None),
    )
    return jax.shard_map(local, mesh=mesh, in_specs=in_specs, out_specs=out_specs, check_vma=False)
```

```python
import math

import jax
import jax.numpy as jnp
from jax import lax
from jax.sharding import Mesh
from jax.sharding import PartitionSpec as P

KRYLOV = 4


epsilon = 1e-06
time_step = 0.1
compress = 0.5
inflation = 4.0


CELL = ("cy", "cz")


def cell_sum(values, doubling=False):
    for axis in ("cz", "cy"):
        size = lax.axis_size(axis)
        if not doubling or size & (size - 1):
            values = lax.psum(values, axis)
            continue
        step = 1
        while step < size:
            values = values + lax.ppermute(values, axis, [(i, i ^ step) for i in range(size)])
            step *= 2
    return values


def mobility(sat_field):
    return sat_field * sat_field + 0.5 * (1.0 - sat_field) * (1.0 - sat_field)


def face_pair(perm_low, perm_high, sat_low, sat_high):
    trans = (
        2.0
        * perm_low
        * perm_high
        / (perm_low + perm_high)
        * (0.5 * (mobility(sat_low) + mobility(sat_high)))
    )
    return (trans, trans * (0.5 * (sat_low + sat_high)))


def plane_faces(perm, sat_field):
    plane_rows = perm.shape[-2]
    plane_cols = perm.shape[-1]
    keep_rows = (
        lax.broadcasted_iota(jnp.int32, (plane_rows, plane_cols), 0) < plane_rows - 1
    ).astype(jnp.float32)
    keep_cols = (
        lax.broadcasted_iota(jnp.int32, (plane_rows, plane_cols), 1) < plane_cols - 1
    ).astype(jnp.float32)
    trans_y, frac_y = face_pair(
        perm, jnp.roll(perm, -1, -2), sat_field, jnp.roll(sat_field, -1, -2)
    )
    trans_z, frac_z = face_pair(
        perm, jnp.roll(perm, -1, -1), sat_field, jnp.roll(sat_field, -1, -1)
    )
    return (trans_y * keep_rows, frac_y * keep_rows, trans_z * keep_cols, frac_z * keep_cols)


def operator(padded, second, coeffs):
    accum, trans_x, frac_x, trans_y, frac_y, trans_z, frac_z = coeffs
    first = padded[..., 1:-1, :, :]
    diff_x = padded[..., 1:, :, :] - padded[..., :-1, :, :]
    diff_y = jnp.roll(first, -1, -2) - first
    diff_z = jnp.roll(first, -1, -1) - first

    def net(coef_x, coef_y, coef_z):
        flow_x = coef_x * diff_x
        flow_y = coef_y * diff_y
        flow_z = coef_z * diff_z
        return (
            flow_x[..., :-1, :, :]
            - flow_x[..., 1:, :, :]
            + (jnp.roll(flow_y, 1, -2) - flow_y)
            + (jnp.roll(flow_z, 1, -1) - flow_z)
        )

    out_pressure = accum * (compress * first + 0.5 * second) + net(trans_x, trans_y, trans_z)
    out_water = accum * second + net(frac_x, frac_y, frac_z)
    return (out_pressure, out_water)


def least_squares(columns, beta):
    rows = [list(column) for column in columns]
    cosines = []
    sines = []
    target = [beta] + [jnp.zeros_like(beta) for column in columns]
    for jdx in range(len(rows)):
        column = rows[jdx]
        for idx in range(jdx):
            upper = cosines[idx] * column[idx] + sines[idx] * column[idx + 1]
            column[idx + 1] = -sines[idx] * column[idx] + cosines[idx] * column[idx + 1]
            column[idx] = upper
        radius = jnp.sqrt(column[jdx] * column[jdx] + column[jdx + 1] * column[jdx + 1])
        cosines.append(column[jdx] / radius)
        sines.append(column[jdx + 1] / radius)
        column[jdx] = radius
        target[jdx + 1] = -sines[jdx] * target[jdx]
        target[jdx] = cosines[jdx] * target[jdx]
    count = len(rows)
    solved = [None] * count
    for jdx in reversed(range(count)):
        partial_sum = target[jdx]
        for idx in range(jdx + 1, count):
            partial_sum = partial_sum - rows[idx][jdx] * solved[idx]
        solved[jdx] = partial_sum / rows[jdx][jdx]
    return solved


def ensemble_weights(predicted, obs_values, obs_error, noise, offset, count):
    members = predicted.shape[0]
    sigma = math.sqrt(inflation) * obs_error
    center = jnp.mean(predicted, axis=0)
    spread = (predicted - center) / (math.sqrt(members - 1.0) * sigma)
    innov = (obs_values + sigma * noise - predicted) / sigma
    own_innov = lax.dynamic_slice_in_dim(innov, offset, count, 0)
    gram = jnp.eye(members, dtype=jnp.float32) + jnp.dot(
        spread, spread.T, precision=lax.Precision.HIGHEST, preferred_element_type=jnp.float32
    )
    cross = jnp.dot(
        spread, own_innov.T, precision=lax.Precision.HIGHEST, preferred_element_type=jnp.float32
    )
    factor = jnp.linalg.cholesky(gram)
    return jax.scipy.linalg.cho_solve((factor, True), cross)


def expand(values):
    return values[:, None, None, None, None]


def inner(left, right):
    return jnp.sum(left * right, axis=(1, 2, 3, 4))


def local(
    rhs, log_perm, porosity, saturation, pressure, obs_values, obs_error, noise, well_cell, obs_well
):
    local_members, slab_x, plane_rows, plane_cols = log_perm.shape
    members = noise.shape[0]
    plane = plane_rows * plane_cols
    cells_dev = slab_x * plane
    slab_index = lax.axis_index("cy") * lax.axis_size("cz") + lax.axis_index("cz")
    slab_count = lax.axis_size("cy") * lax.axis_size("cz")
    count = slab_count
    forward = [(i, i + 1) for i in range(count - 1)]
    backward = [(target, source) for source, target in forward]
    edges = (log_perm, saturation, rhs[:, 0])
    low = lax.ppermute(jnp.stack([field[:, -1:] for field in edges], 1), CELL, forward)
    high = lax.ppermute(jnp.stack([field[:, :1] for field in edges], 1), CELL, backward)
    perm_pad = jnp.exp(jnp.concatenate([low[:, 0], log_perm, high[:, 0]], axis=1))
    sat_pad = jnp.concatenate([low[:, 1], saturation, high[:, 1]], axis=1)
    trans_x, frac_x = face_pair(perm_pad[:, :-1], perm_pad[:, 1:], sat_pad[:, :-1], sat_pad[:, 1:])
    face_pos = lax.broadcasted_iota(jnp.int32, (slab_x + 1, 1, 1), 0)
    keep_face = jnp.where(
        face_pos == 0,
        slab_index > 0,
        jnp.where(face_pos == slab_x, slab_index < slab_count - 1, True),
    ).astype(jnp.float32)
    trans_x = trans_x * keep_face
    frac_x = frac_x * keep_face
    trans_y, frac_y, trans_z, frac_z = plane_faces(perm_pad[:, 1:-1], saturation)
    coeffs = (porosity / time_step, trans_x, frac_x, trans_y, frac_y, trans_z, frac_z)

    def planes(field):
        low = lax.ppermute(field[:, -1:], CELL, forward)
        high = lax.ppermute(field[:, :1], CELL, backward)
        return (low, high)

    def apply(vector, ghosts):
        padded = jnp.concatenate([ghosts[0], vector[:, 0], ghosts[1]], axis=1)
        out_pressure, out_water = operator(padded, vector[:, 1], coeffs)
        return jnp.stack([out_pressure, out_water], 1)

    def scale_planes(ghosts, scale):
        factor = scale[:, None, None, None]
        return (ghosts[0] / factor, ghosts[1] / factor)

    rhs_planes = (low[:, 2], high[:, 2])
    image = apply(rhs, rhs_planes)
    parts = jnp.stack([inner(rhs, rhs), inner(rhs, image)], 0)
    image_planes = planes(image[:, 0])
    reduced = cell_sum(parts)
    beta = jnp.sqrt(reduced[0] + epsilon)
    basis = [rhs / expand(beta)]
    basis_planes = [scale_planes(rhs_planes, beta)]
    image = image / expand(beta)
    image_planes = scale_planes(image_planes, beta)
    projected = [reduced[1] / (beta * beta)]
    columns = []
    for jdx in range(KRYLOV):
        ortho = image
        ortho_low, ortho_high = image_planes
        for idx in range(jdx + 1):
            ortho = ortho - expand(projected[idx]) * basis[idx]
            factor = projected[idx][:, None, None, None]
            ortho_low = ortho_low - factor * basis_planes[idx][0]
            ortho_high = ortho_high - factor * basis_planes[idx][1]
        ortho_planes = (ortho_low, ortho_high)
        if jdx == KRYLOV - 1:
            height = jnp.sqrt(cell_sum(inner(ortho, ortho)) + epsilon)
            columns.append(projected + [height])
            break
        image = apply(ortho, ortho_planes)
        parts = [inner(ortho, ortho)]
        parts += [inner(basis[idx], image) for idx in range(jdx + 1)]
        parts.append(inner(ortho, image))
        parts = jnp.stack(parts, 0)
        image_planes = planes(image[:, 0])
        reduced = cell_sum(parts)
        height = jnp.sqrt(reduced[0] + epsilon)
        columns.append(projected + [height])
        basis.append(ortho / expand(height))
        basis_planes.append(scale_planes(ortho_planes, height))
        image = image / expand(height)
        image_planes = scale_planes(image_planes, height)
        projected = [reduced[1 + idx] / height for idx in range(jdx + 1)]
        projected.append(reduced[jdx + 2] / (height * height))
    solved = least_squares(columns, beta)
    increment = expand(solved[0]) * basis[0]
    for jdx in range(1, KRYLOV):
        increment = increment + expand(solved[jdx]) * basis[jdx]
    cells = jnp.take(well_cell, obs_well)
    wells = well_cell.shape[0]
    component = (jnp.arange(obs_well.shape[0], dtype=jnp.int32) >= wells).astype(jnp.int32)
    slab_row = cells // plane - slab_index * slab_x
    inside = (slab_row >= 0) & (slab_row < slab_x)
    rows = 2 * slab_x * plane_rows
    row = component * (slab_x * plane_rows) + slab_row * plane_rows + (cells % plane) // plane_cols
    col_z = cells % plane_cols
    state = jnp.stack([pressure + increment[:, 0], saturation + increment[:, 1]], 1)
    table = state.reshape(local_members * rows, plane_cols)
    pick_z = (lax.broadcasted_iota(jnp.int32, (plane_cols, cells.shape[0]), 0) == col_z[None, :])
    by_row = jnp.dot(
        table,
        pick_z.astype(jnp.float32),
        precision=lax.Precision.HIGHEST,
        preferred_element_type=jnp.float32,
    )
    pick_row = (lax.broadcasted_iota(jnp.int32, (rows, cells.shape[0]), 0) == row[None, :]) & inside[None, :]
    picked = jnp.sum(
        by_row.reshape(local_members, rows, cells.shape[0]) * pick_row.astype(jnp.float32)[None],
        axis=1,
    )
    slab_pred = cell_sum(picked, doubling=True)
    predicted = lax.all_gather(slab_pred, "grp", axis=0, tiled=True)
    params = jnp.stack([log_perm, porosity], 1).reshape(local_members, 2 * cells_dev)
    offset = lax.axis_index("grp") * local_members
    own_columns = ensemble_weights(predicted, obs_values, obs_error, noise, offset, local_members)
    scale_factor = 1.0 / math.sqrt(members - 1.0)
    scaled = params * scale_factor
    update = jnp.dot(
        own_columns.T,
        lax.all_gather(scaled, "grp", axis=0, tiled=True),
        precision=lax.Precision.HIGHEST,
        preferred_element_type=jnp.float32,
    )
    posterior = params + update
    posterior = posterior.reshape(local_members, 2, slab_x, plane_rows, plane_cols)
    return (increment, posterior[:, 0], posterior[:, 1])


def split_mesh(mesh):
    devices = mesh.devices
    groups, slabs = devices.shape
    along_z = len({device.coords[2] for device in devices[0]})
    return Mesh(devices.reshape(groups, slabs // along_z, along_z), ("grp", "cy", "cz"))


def solution(mesh):
    mesh = split_mesh(mesh)
    in_specs = (
        P("grp", None, CELL, None, None),
        P("grp", CELL, None, None),
        P("grp", CELL, None, None),
        P("grp", CELL, None, None),
        P("grp", CELL, None, None),
        P(),
        P(),
        P(),
        P(),
        P(),
    )
    out_specs = (
        P("grp", None, CELL, None, None),
        P("grp", CELL, None, None),
        P("grp", CELL, None, None),
    )
    return jax.shard_map(local, mesh=mesh, in_specs=in_specs, out_specs=out_specs, check_vma=False)
```

```python
import math

import jax
import jax.numpy as jnp
from jax import lax
from jax.sharding import Mesh
from jax.sharding import PartitionSpec as P

KRYLOV = 4


epsilon = 1e-06
time_step = 0.1
compress = 0.5
inflation = 4.0


CELL = ("cy", "cz")


def cell_sum(values, doubling=False):
    for axis in ("cz", "cy"):
        size = lax.axis_size(axis)
        if not doubling or size & (size - 1):
            values = lax.psum(values, axis)
            continue
        step = 1
        while step < size:
            values = values + lax.ppermute(values, axis, [(i, i ^ step) for i in range(size)])
            step *= 2
    return values


def mobility(sat_field):
    return sat_field * sat_field + 0.5 * (1.0 - sat_field) * (1.0 - sat_field)


def face_pair(perm_low, perm_high, sat_low, sat_high):
    trans = (
        2.0
        * perm_low
        * perm_high
        / (perm_low + perm_high)
        * (0.5 * (mobility(sat_low) + mobility(sat_high)))
    )
    return (trans, trans * (0.5 * (sat_low + sat_high)))


def plane_faces(perm, sat_field):
    plane_rows = perm.shape[-2]
    plane_cols = perm.shape[-1]
    keep_rows = (
        lax.broadcasted_iota(jnp.int32, (plane_rows, plane_cols), 0) < plane_rows - 1
    ).astype(jnp.float32)
    keep_cols = (
        lax.broadcasted_iota(jnp.int32, (plane_rows, plane_cols), 1) < plane_cols - 1
    ).astype(jnp.float32)
    trans_y, frac_y = face_pair(
        perm, jnp.roll(perm, -1, -2), sat_field, jnp.roll(sat_field, -1, -2)
    )
    trans_z, frac_z = face_pair(
        perm, jnp.roll(perm, -1, -1), sat_field, jnp.roll(sat_field, -1, -1)
    )
    return (trans_y * keep_rows, frac_y * keep_rows, trans_z * keep_cols, frac_z * keep_cols)


def operator(padded, second, coeffs):
    accum, trans_x, frac_x, trans_y, frac_y, trans_z, frac_z = coeffs
    first = padded[..., 1:-1, :, :]
    diff_x = padded[..., 1:, :, :] - padded[..., :-1, :, :]
    diff_y = jnp.roll(first, -1, -2) - first
    diff_z = jnp.roll(first, -1, -1) - first

    def net(coef_x, coef_y, coef_z):
        flow_x = coef_x * diff_x
        flow_y = coef_y * diff_y
        flow_z = coef_z * diff_z
        return (
            flow_x[..., :-1, :, :]
            - flow_x[..., 1:, :, :]
            + (jnp.roll(flow_y, 1, -2) - flow_y)
            + (jnp.roll(flow_z, 1, -1) - flow_z)
        )

    out_pressure = accum * (compress * first + 0.5 * second) + net(trans_x, trans_y, trans_z)
    out_water = accum * second + net(frac_x, frac_y, frac_z)
    return (out_pressure, out_water)


def least_squares(columns, beta):
    rows = [list(column) for column in columns]
    cosines = []
    sines = []
    target = [beta] + [jnp.zeros_like(beta) for column in columns]
    for jdx in range(len(rows)):
        column = rows[jdx]
        for idx in range(jdx):
            upper = cosines[idx] * column[idx] + sines[idx] * column[idx + 1]
            column[idx + 1] = -sines[idx] * column[idx] + cosines[idx] * column[idx + 1]
            column[idx] = upper
        radius = jnp.sqrt(column[jdx] * column[jdx] + column[jdx + 1] * column[jdx + 1])
        cosines.append(column[jdx] / radius)
        sines.append(column[jdx + 1] / radius)
        column[jdx] = radius
        target[jdx + 1] = -sines[jdx] * target[jdx]
        target[jdx] = cosines[jdx] * target[jdx]
    count = len(rows)
    solved = [None] * count
    for jdx in reversed(range(count)):
        partial_sum = target[jdx]
        for idx in range(jdx + 1, count):
            partial_sum = partial_sum - rows[idx][jdx] * solved[idx]
        solved[jdx] = partial_sum / rows[jdx][jdx]
    return solved


def ensemble_weights(predicted, obs_values, obs_error, noise, offset, count):
    members = predicted.shape[0]
    sigma = math.sqrt(inflation) * obs_error
    center = jnp.mean(predicted, axis=0)
    spread = (predicted - center) / (math.sqrt(members - 1.0) * sigma)
    innov = (obs_values + sigma * noise - predicted) / sigma
    own_innov = lax.dynamic_slice_in_dim(innov, offset, count, 0)
    gram = jnp.eye(members, dtype=jnp.float32) + jnp.dot(
        spread, spread.T, precision=lax.Precision.HIGHEST, preferred_element_type=jnp.float32
    )
    cross = jnp.dot(
        spread, own_innov.T, precision=lax.Precision.HIGHEST, preferred_element_type=jnp.float32
    )
    factor = jnp.linalg.cholesky(gram)
    return jax.scipy.linalg.cho_solve((factor, True), cross)


def expand(values):
    return values[:, None, None, None, None]


def inner(left, right):
    return jnp.sum(left * right, axis=(1, 2, 3, 4))


def local(
    rhs, log_perm, porosity, saturation, pressure, obs_values, obs_error, noise, well_cell, obs_well
):
    local_members, slab_x, plane_rows, plane_cols = log_perm.shape
    members = noise.shape[0]
    plane = plane_rows * plane_cols
    cells_dev = slab_x * plane
    slab_index = lax.axis_index("cy") * lax.axis_size("cz") + lax.axis_index("cz")
    slab_count = lax.axis_size("cy") * lax.axis_size("cz")
    count = slab_count
    forward = [(i, i + 1) for i in range(count - 1)]
    backward = [(target, source) for source, target in forward]
    edges = (log_perm, saturation, rhs[:, 0])
    low = lax.ppermute(jnp.stack([field[:, -1:] for field in edges], 1), CELL, forward)
    high = lax.ppermute(jnp.stack([field[:, :1] for field in edges], 1), CELL, backward)
    perm_pad = jnp.exp(jnp.concatenate([low[:, 0], log_perm, high[:, 0]], axis=1))
    sat_pad = jnp.concatenate([low[:, 1], saturation, high[:, 1]], axis=1)
    trans_x, frac_x = face_pair(perm_pad[:, :-1], perm_pad[:, 1:], sat_pad[:, :-1], sat_pad[:, 1:])
    face_pos = lax.broadcasted_iota(jnp.int32, (slab_x + 1, 1, 1), 0)
    keep_face = jnp.where(
        face_pos == 0,
        slab_index > 0,
        jnp.where(face_pos == slab_x, slab_index < slab_count - 1, True),
    ).astype(jnp.float32)
    trans_x = trans_x * keep_face
    frac_x = frac_x * keep_face
    trans_y, frac_y, trans_z, frac_z = plane_faces(perm_pad[:, 1:-1], saturation)
    coeffs = (porosity / time_step, trans_x, frac_x, trans_y, frac_y, trans_z, frac_z)

    def planes(field):
        low = lax.ppermute(field[:, -1:], CELL, forward)
        high = lax.ppermute(field[:, :1], CELL, backward)
        return (low, high)

    def apply(vector, ghosts):
        padded = jnp.concatenate([ghosts[0], vector[:, 0], ghosts[1]], axis=1)
        out_pressure, out_water = operator(padded, vector[:, 1], coeffs)
        return jnp.stack([out_pressure, out_water], 1)

    def scale_planes(ghosts, scale):
        factor = scale[:, None, None, None]
        return (ghosts[0] / factor, ghosts[1] / factor)

    rhs_planes = (low[:, 2], high[:, 2])
    image = apply(rhs, rhs_planes)
    parts = jnp.stack([inner(rhs, rhs), inner(rhs, image)], 0)
    image_planes = planes(image[:, 0])
    reduced = cell_sum(parts)
    beta = jnp.sqrt(reduced[0] + epsilon)
    basis = [rhs / expand(beta)]
    basis_planes = [scale_planes(rhs_planes, beta)]
    image = image / expand(beta)
    image_planes = scale_planes(image_planes, beta)
    projected = [reduced[1] / (beta * beta)]
    columns = []
    for jdx in range(KRYLOV):
        ortho = image
        ortho_low, ortho_high = image_planes
        for idx in range(jdx + 1):
            ortho = ortho - expand(projected[idx]) * basis[idx]
            factor = projected[idx][:, None, None, None]
            ortho_low = ortho_low - factor * basis_planes[idx][0]
            ortho_high = ortho_high - factor * basis_planes[idx][1]
        ortho_planes = (ortho_low, ortho_high)
        if jdx == KRYLOV - 1:
            height = jnp.sqrt(cell_sum(inner(ortho, ortho)) + epsilon)
            columns.append(projected + [height])
            break
        image = apply(ortho, ortho_planes)
        parts = [inner(ortho, ortho)]
        parts += [inner(basis[idx], image) for idx in range(jdx + 1)]
        parts.append(inner(ortho, image))
        parts = jnp.stack(parts, 0)
        image_planes = planes(image[:, 0])
        reduced = cell_sum(parts)
        height = jnp.sqrt(reduced[0] + epsilon)
        columns.append(projected + [height])
        basis.append(ortho / expand(height))
        basis_planes.append(scale_planes(ortho_planes, height))
        image = image / expand(height)
        image_planes = scale_planes(image_planes, height)
        projected = [reduced[1 + idx] / height for idx in range(jdx + 1)]
        projected.append(reduced[jdx + 2] / (height * height))
    solved = least_squares(columns, beta)
    increment = expand(solved[0]) * basis[0]
    for jdx in range(1, KRYLOV):
        increment = increment + expand(solved[jdx]) * basis[jdx]
    cells = jnp.take(well_cell, obs_well)
    wells = well_cell.shape[0]
    component = (jnp.arange(obs_well.shape[0], dtype=jnp.int32) >= wells).astype(jnp.int32)
    slab_row = cells // plane - slab_index * slab_x
    inside = (slab_row >= 0) & (slab_row < slab_x)
    rows = 2 * slab_x * plane_rows
    row = component * (slab_x * plane_rows) + slab_row * plane_rows + (cells % plane) // plane_cols
    col_z = cells % plane_cols
    state = jnp.stack([pressure + increment[:, 0], saturation + increment[:, 1]], 1)
    table = state.reshape(local_members * rows, plane_cols)
    pick_z = (lax.broadcasted_iota(jnp.int32, (plane_cols, cells.shape[0]), 0) == col_z[None, :])
    by_row = jnp.dot(
        table,
        pick_z.astype(jnp.float32),
        precision=lax.Precision.HIGHEST,
        preferred_element_type=jnp.float32,
    )
    pick_row = (lax.broadcasted_iota(jnp.int32, (rows, cells.shape[0]), 0) == row[None, :]) & inside[None, :]
    picked = jnp.sum(
        by_row.reshape(local_members, rows, cells.shape[0]) * pick_row.astype(jnp.float32)[None],
        axis=1,
    )
    slab_pred = cell_sum(picked, doubling=True)
    predicted = lax.all_gather(slab_pred, "grp", axis=0, tiled=True)
    params = jnp.stack([log_perm, porosity], 1).reshape(local_members, 2 * cells_dev)
    offset = lax.axis_index("grp") * local_members
    own_columns = ensemble_weights(predicted, obs_values, obs_error, noise, offset, local_members)
    scale_factor = 1.0 / math.sqrt(members - 1.0)
    update = jnp.dot(
        own_columns.T * scale_factor,
        lax.all_gather(params, "grp", axis=0, tiled=True),
        precision=lax.Precision.HIGHEST,
        preferred_element_type=jnp.float32,
    )
    posterior = params + update
    posterior = posterior.reshape(local_members, 2, slab_x, plane_rows, plane_cols)
    return (increment, posterior[:, 0], posterior[:, 1])


def split_mesh(mesh):
    devices = mesh.devices
    groups, slabs = devices.shape
    along_z = len({device.coords[2] for device in devices[0]})
    return Mesh(devices.reshape(groups, slabs // along_z, along_z), ("grp", "cy", "cz"))


def solution(mesh):
    mesh = split_mesh(mesh)
    in_specs = (
        P("grp", None, CELL, None, None),
        P("grp", CELL, None, None),
        P("grp", CELL, None, None),
        P("grp", CELL, None, None),
        P("grp", CELL, None, None),
        P(),
        P(),
        P(),
        P(),
        P(),
    )
    out_specs = (
        P("grp", None, CELL, None, None),
        P("grp", CELL, None, None),
        P("grp", CELL, None, None),
    )
    return jax.shard_map(local, mesh=mesh, in_specs=in_specs, out_specs=out_specs, check_vma=False)
```

```python
import math

import jax
import jax.numpy as jnp
from jax import lax
from jax.sharding import Mesh
from jax.sharding import PartitionSpec as P

KRYLOV = 4


epsilon = 1e-06
time_step = 0.1
compress = 0.5
inflation = 4.0


CELL = ("cy", "cz")


def cell_sum(values, doubling=False):
    for axis in ("cz", "cy"):
        size = lax.axis_size(axis)
        if not doubling or size & (size - 1):
            values = lax.psum(values, axis)
            continue
        step = 1
        while step < size:
            values = values + lax.ppermute(values, axis, [(i, i ^ step) for i in range(size)])
            step *= 2
    return values


def mobility(sat_field):
    return sat_field * sat_field + 0.5 * (1.0 - sat_field) * (1.0 - sat_field)


def face_pair(perm_low, perm_high, sat_low, sat_high):
    trans = (
        2.0
        * perm_low
        * perm_high
        / (perm_low + perm_high)
        * (0.5 * (mobility(sat_low) + mobility(sat_high)))
    )
    return (trans, trans * (0.5 * (sat_low + sat_high)))


def plane_faces(perm, sat_field):
    plane_rows = perm.shape[-2]
    plane_cols = perm.shape[-1]
    keep_rows = (
        lax.broadcasted_iota(jnp.int32, (plane_rows, plane_cols), 0) < plane_rows - 1
    ).astype(jnp.float32)
    keep_cols = (
        lax.broadcasted_iota(jnp.int32, (plane_rows, plane_cols), 1) < plane_cols - 1
    ).astype(jnp.float32)
    trans_y, frac_y = face_pair(
        perm, jnp.roll(perm, -1, -2), sat_field, jnp.roll(sat_field, -1, -2)
    )
    trans_z, frac_z = face_pair(
        perm, jnp.roll(perm, -1, -1), sat_field, jnp.roll(sat_field, -1, -1)
    )
    return (trans_y * keep_rows, frac_y * keep_rows, trans_z * keep_cols, frac_z * keep_cols)


def operator(padded, second, coeffs):
    accum, trans_x, frac_x, trans_y, frac_y, trans_z, frac_z = coeffs
    first = padded[..., 1:-1, :, :]
    diff_x = padded[..., 1:, :, :] - padded[..., :-1, :, :]
    diff_y = jnp.roll(first, -1, -2) - first
    diff_z = jnp.roll(first, -1, -1) - first

    def net(coef_x, coef_y, coef_z):
        flow_x = coef_x * diff_x
        flow_y = coef_y * diff_y
        flow_z = coef_z * diff_z
        return (
            flow_x[..., :-1, :, :]
            - flow_x[..., 1:, :, :]
            + (jnp.roll(flow_y, 1, -2) - flow_y)
            + (jnp.roll(flow_z, 1, -1) - flow_z)
        )

    out_pressure = accum * (compress * first + 0.5 * second) + net(trans_x, trans_y, trans_z)
    out_water = accum * second + net(frac_x, frac_y, frac_z)
    return (out_pressure, out_water)


def least_squares(columns, beta):
    rows = [list(column) for column in columns]
    cosines = []
    sines = []
    target = [beta] + [jnp.zeros_like(beta) for column in columns]
    for jdx in range(len(rows)):
        column = rows[jdx]
        for idx in range(jdx):
            upper = cosines[idx] * column[idx] + sines[idx] * column[idx + 1]
            column[idx + 1] = -sines[idx] * column[idx] + cosines[idx] * column[idx + 1]
            column[idx] = upper
        radius = jnp.sqrt(column[jdx] * column[jdx] + column[jdx + 1] * column[jdx + 1])
        cosines.append(column[jdx] / radius)
        sines.append(column[jdx + 1] / radius)
        column[jdx] = radius
        target[jdx + 1] = -sines[jdx] * target[jdx]
        target[jdx] = cosines[jdx] * target[jdx]
    count = len(rows)
    solved = [None] * count
    for jdx in reversed(range(count)):
        partial_sum = target[jdx]
        for idx in range(jdx + 1, count):
            partial_sum = partial_sum - rows[idx][jdx] * solved[idx]
        solved[jdx] = partial_sum / rows[jdx][jdx]
    return solved


def ensemble_weights(predicted, obs_values, obs_error, noise, offset, count):
    members = predicted.shape[0]
    sigma = math.sqrt(inflation) * obs_error
    center = jnp.mean(predicted, axis=0)
    spread = (predicted - center) / (math.sqrt(members - 1.0) * sigma)
    innov = (obs_values + sigma * noise - predicted) / sigma
    own_innov = lax.dynamic_slice_in_dim(innov, offset, count, 0)
    gram = jnp.eye(members, dtype=jnp.float32) + jnp.dot(
        spread, spread.T, precision=lax.Precision.HIGHEST, preferred_element_type=jnp.float32
    )
    cross = jnp.dot(
        spread, own_innov.T, precision=lax.Precision.HIGHEST, preferred_element_type=jnp.float32
    )
    factor = jnp.linalg.cholesky(gram)
    return jax.scipy.linalg.cho_solve((factor, True), cross)


def expand(values):
    return values[:, None, None, None, None]


def inner(left, right):
    return jnp.sum(left * right, axis=(1, 2, 3, 4))


def local(
    rhs, log_perm, porosity, saturation, pressure, obs_values, obs_error, noise, well_cell, obs_well
):
    local_members, slab_x, plane_rows, plane_cols = log_perm.shape
    members = noise.shape[0]
    plane = plane_rows * plane_cols
    cells_dev = slab_x * plane
    slab_index = lax.axis_index("cy") * lax.axis_size("cz") + lax.axis_index("cz")
    slab_count = lax.axis_size("cy") * lax.axis_size("cz")
    cells = jnp.take(well_cell, obs_well)
    wells = well_cell.shape[0]
    nobs = cells.shape[0]
    component = (jnp.arange(nobs, dtype=jnp.int32) >= wells).astype(jnp.int32)
    slab_row = cells // plane - slab_index * slab_x
    inside = (slab_row >= 0) & (slab_row < slab_x)
    rows = 2 * slab_x * plane_rows
    row = component * (slab_x * plane_rows) + slab_row * plane_rows + (cells % plane) // plane_cols
    col_z = cells % plane_cols
    pick_z = (lax.broadcasted_iota(jnp.int32, (plane_cols, nobs), 0) == col_z[None, :]).astype(jnp.float32)
    pick_row = (lax.broadcasted_iota(jnp.int32, (rows, nobs), 0) == row[None, :]) & inside[None, :]
    pick_row = pick_row.astype(jnp.float32)

    def pick(field):
        by_row = jnp.dot(
            field.reshape(local_members * rows, plane_cols),
            pick_z,
            precision=lax.Precision.HIGHEST,
            preferred_element_type=jnp.float32,
        )
        return jnp.sum(by_row.reshape(local_members, rows, nobs) * pick_row[None], axis=1)

    count = slab_count
    forward = [(i, i + 1) for i in range(count - 1)]
    backward = [(target, source) for source, target in forward]
    edges = (log_perm, saturation, rhs[:, 0])
    low = lax.ppermute(jnp.stack([field[:, -1:] for field in edges], 1), CELL, forward)
    high = lax.ppermute(jnp.stack([field[:, :1] for field in edges], 1), CELL, backward)
    perm_pad = jnp.exp(jnp.concatenate([low[:, 0], log_perm, high[:, 0]], axis=1))
    sat_pad = jnp.concatenate([low[:, 1], saturation, high[:, 1]], axis=1)
    trans_x, frac_x = face_pair(perm_pad[:, :-1], perm_pad[:, 1:], sat_pad[:, :-1], sat_pad[:, 1:])
    face_pos = lax.broadcasted_iota(jnp.int32, (slab_x + 1, 1, 1), 0)
    keep_face = jnp.where(
        face_pos == 0,
        slab_index > 0,
        jnp.where(face_pos == slab_x, slab_index < slab_count - 1, True),
    ).astype(jnp.float32)
    trans_x = trans_x * keep_face
    frac_x = frac_x * keep_face
    trans_y, frac_y, trans_z, frac_z = plane_faces(perm_pad[:, 1:-1], saturation)
    coeffs = (porosity / time_step, trans_x, frac_x, trans_y, frac_y, trans_z, frac_z)

    def planes(field):
        low = lax.ppermute(field[:, -1:], CELL, forward)
        high = lax.ppermute(field[:, :1], CELL, backward)
        return (low, high)

    def apply(vector, ghosts):
        padded = jnp.concatenate([ghosts[0], vector[:, 0], ghosts[1]], axis=1)
        out_pressure, out_water = operator(padded, vector[:, 1], coeffs)
        return jnp.stack([out_pressure, out_water], 1)

    def scale_planes(ghosts, scale):
        factor = scale[:, None, None, None]
        return (ghosts[0] / factor, ghosts[1] / factor)

    rhs_planes = (low[:, 2], high[:, 2])
    image = apply(rhs, rhs_planes)
    parts = jnp.stack([inner(rhs, rhs), inner(rhs, image)], 0)
    image_planes = planes(image[:, 0])
    reduced = cell_sum(parts)
    beta = jnp.sqrt(reduced[0] + epsilon)
    basis = [rhs / expand(beta)]
    basis_planes = [scale_planes(rhs_planes, beta)]
    image = image / expand(beta)
    image_planes = scale_planes(image_planes, beta)
    projected = [reduced[1] / (beta * beta)]
    columns = []
    for jdx in range(KRYLOV):
        ortho = image
        ortho_low, ortho_high = image_planes
        for idx in range(jdx + 1):
            ortho = ortho - expand(projected[idx]) * basis[idx]
            factor = projected[idx][:, None, None, None]
            ortho_low = ortho_low - factor * basis_planes[idx][0]
            ortho_high = ortho_high - factor * basis_planes[idx][1]
        ortho_planes = (ortho_low, ortho_high)
        if jdx == KRYLOV - 1:
            state = jnp.stack([pressure, saturation], 1)
            payload = [inner(ortho, ortho)[:, None], pick(state)]
            payload += [pick(basis[idx]) for idx in range(KRYLOV)]
            reduced = cell_sum(jnp.concatenate(payload, 1), doubling=True)
            height = jnp.sqrt(reduced[:, 0] + epsilon)
            columns.append(projected + [height])
            picks = [reduced[:, 1 + nobs * idx : 1 + nobs * (idx + 1)] for idx in range(KRYLOV + 1)]
            break
        image = apply(ortho, ortho_planes)
        parts = [inner(ortho, ortho)]
        parts += [inner(basis[idx], image) for idx in range(jdx + 1)]
        parts.append(inner(ortho, image))
        parts = jnp.stack(parts, 0)
        image_planes = planes(image[:, 0])
        reduced = cell_sum(parts)
        height = jnp.sqrt(reduced[0] + epsilon)
        columns.append(projected + [height])
        basis.append(ortho / expand(height))
        basis_planes.append(scale_planes(ortho_planes, height))
        image = image / expand(height)
        image_planes = scale_planes(image_planes, height)
        projected = [reduced[1 + idx] / height for idx in range(jdx + 1)]
        projected.append(reduced[jdx + 2] / (height * height))
    solved = least_squares(columns, beta)
    increment = expand(solved[0]) * basis[0]
    at_wells = solved[0][:, None] * picks[1]
    for jdx in range(1, KRYLOV):
        increment = increment + expand(solved[jdx]) * basis[jdx]
        at_wells = at_wells + solved[jdx][:, None] * picks[1 + jdx]
    slab_pred = picks[0] + at_wells
    predicted = lax.all_gather(slab_pred, "grp", axis=0, tiled=True)
    params = jnp.stack([log_perm, porosity], 1).reshape(local_members, 2 * cells_dev)
    offset = lax.axis_index("grp") * local_members
    own_columns = ensemble_weights(predicted, obs_values, obs_error, noise, offset, local_members)
    scale_factor = 1.0 / math.sqrt(members - 1.0)
    scaled = params * scale_factor
    update = jnp.dot(
        own_columns.T,
        lax.all_gather(scaled, "grp", axis=0, tiled=True),
        precision=lax.Precision.HIGHEST,
        preferred_element_type=jnp.float32,
    )
    posterior = params + update
    posterior = posterior.reshape(local_members, 2, slab_x, plane_rows, plane_cols)
    return (increment, posterior[:, 0], posterior[:, 1])


def split_mesh(mesh):
    devices = mesh.devices
    groups, slabs = devices.shape
    along_z = len({device.coords[2] for device in devices[0]})
    return Mesh(devices.reshape(groups, slabs // along_z, along_z), ("grp", "cy", "cz"))


def solution(mesh):
    mesh = split_mesh(mesh)
    in_specs = (
        P("grp", None, CELL, None, None),
        P("grp", CELL, None, None),
        P("grp", CELL, None, None),
        P("grp", CELL, None, None),
        P("grp", CELL, None, None),
        P(),
        P(),
        P(),
        P(),
        P(),
    )
    out_specs = (
        P("grp", None, CELL, None, None),
        P("grp", CELL, None, None),
        P("grp", CELL, None, None),
    )
    return jax.shard_map(local, mesh=mesh, in_specs=in_specs, out_specs=out_specs, check_vma=False)
```

```python
import math

import jax
import jax.numpy as jnp
from jax import lax
from jax.sharding import Mesh
from jax.sharding import PartitionSpec as P

KRYLOV = 4


epsilon = 1e-06
time_step = 0.1
compress = 0.5
inflation = 4.0


CELL = ("cy", "cz")


def cell_sum(values, doubling=False):
    for axis in ("cz", "cy"):
        size = lax.axis_size(axis)
        if not doubling or size & (size - 1):
            values = lax.psum(values, axis)
            continue
        step = 1
        while step < size:
            values = values + lax.ppermute(values, axis, [(i, i ^ step) for i in range(size)])
            step *= 2
    return values


def mobility(sat_field):
    return sat_field * sat_field + 0.5 * (1.0 - sat_field) * (1.0 - sat_field)


def face_pair(perm_low, perm_high, sat_low, sat_high):
    trans = (
        2.0
        * perm_low
        * perm_high
        / (perm_low + perm_high)
        * (0.5 * (mobility(sat_low) + mobility(sat_high)))
    )
    return (trans, trans * (0.5 * (sat_low + sat_high)))


def plane_faces(perm, sat_field):
    plane_rows = perm.shape[-2]
    plane_cols = perm.shape[-1]
    keep_rows = (
        lax.broadcasted_iota(jnp.int32, (plane_rows, plane_cols), 0) < plane_rows - 1
    ).astype(jnp.float32)
    keep_cols = (
        lax.broadcasted_iota(jnp.int32, (plane_rows, plane_cols), 1) < plane_cols - 1
    ).astype(jnp.float32)
    trans_y, frac_y = face_pair(
        perm, jnp.roll(perm, -1, -2), sat_field, jnp.roll(sat_field, -1, -2)
    )
    trans_z, frac_z = face_pair(
        perm, jnp.roll(perm, -1, -1), sat_field, jnp.roll(sat_field, -1, -1)
    )
    return (trans_y * keep_rows, frac_y * keep_rows, trans_z * keep_cols, frac_z * keep_cols)


def operator(padded, second, coeffs):
    accum, trans_x, frac_x, trans_y, frac_y, trans_z, frac_z = coeffs
    first = padded[..., 1:-1, :, :]
    diff_x = padded[..., 1:, :, :] - padded[..., :-1, :, :]
    diff_y = jnp.roll(first, -1, -2) - first
    diff_z = jnp.roll(first, -1, -1) - first

    def net(coef_x, coef_y, coef_z):
        flow_x = coef_x * diff_x
        flow_y = coef_y * diff_y
        flow_z = coef_z * diff_z
        return (
            flow_x[..., :-1, :, :]
            - flow_x[..., 1:, :, :]
            + (jnp.roll(flow_y, 1, -2) - flow_y)
            + (jnp.roll(flow_z, 1, -1) - flow_z)
        )

    out_pressure = accum * (compress * first + 0.5 * second) + net(trans_x, trans_y, trans_z)
    out_water = accum * second + net(frac_x, frac_y, frac_z)
    return (out_pressure, out_water)


def least_squares(columns, beta):
    rows = [list(column) for column in columns]
    cosines = []
    sines = []
    target = [beta] + [jnp.zeros_like(beta) for column in columns]
    for jdx in range(len(rows)):
        column = rows[jdx]
        for idx in range(jdx):
            upper = cosines[idx] * column[idx] + sines[idx] * column[idx + 1]
            column[idx + 1] = -sines[idx] * column[idx] + cosines[idx] * column[idx + 1]
            column[idx] = upper
        radius = jnp.sqrt(column[jdx] * column[jdx] + column[jdx + 1] * column[jdx + 1])
        cosines.append(column[jdx] / radius)
        sines.append(column[jdx + 1] / radius)
        column[jdx] = radius
        target[jdx + 1] = -sines[jdx] * target[jdx]
        target[jdx] = cosines[jdx] * target[jdx]
    count = len(rows)
    solved = [None] * count
    for jdx in reversed(range(count)):
        partial_sum = target[jdx]
        for idx in range(jdx + 1, count):
            partial_sum = partial_sum - rows[idx][jdx] * solved[idx]
        solved[jdx] = partial_sum / rows[jdx][jdx]
    return solved


def ensemble_weights(predicted, obs_values, obs_error, noise, offset, count):
    members = predicted.shape[0]
    sigma = math.sqrt(inflation) * obs_error
    center = jnp.mean(predicted, axis=0)
    spread = (predicted - center) / (math.sqrt(members - 1.0) * sigma)
    innov = (obs_values + sigma * noise - predicted) / sigma
    own_innov = lax.dynamic_slice_in_dim(innov, offset, count, 0)
    gram = jnp.eye(members, dtype=jnp.float32) + jnp.dot(
        spread, spread.T, precision=lax.Precision.HIGHEST, preferred_element_type=jnp.float32
    )
    cross = jnp.dot(
        spread, own_innov.T, precision=lax.Precision.HIGHEST, preferred_element_type=jnp.float32
    )
    factor = jnp.linalg.cholesky(gram)
    return jax.scipy.linalg.cho_solve((factor, True), cross)


def expand(values):
    return values[:, None, None, None, None]


def inner(left, right):
    return jnp.sum(left * right, axis=(1, 2, 3, 4))


def local(
    rhs, log_perm, porosity, saturation, pressure, obs_values, obs_error, noise, well_cell, obs_well
):
    local_members, slab_x, plane_rows, plane_cols = log_perm.shape
    members = noise.shape[0]
    plane = plane_rows * plane_cols
    cells_dev = slab_x * plane
    slab_index = lax.axis_index("cy") * lax.axis_size("cz") + lax.axis_index("cz")
    slab_count = lax.axis_size("cy") * lax.axis_size("cz")
    count = slab_count
    forward = [(i, i + 1) for i in range(count - 1)]
    backward = [(target, source) for source, target in forward]
    edges = (log_perm, saturation, rhs[:, 0])
    low = lax.ppermute(jnp.stack([field[:, -1:] for field in edges], 1), CELL, forward)
    high = lax.ppermute(jnp.stack([field[:, :1] for field in edges], 1), CELL, backward)
    perm_pad = jnp.exp(jnp.concatenate([low[:, 0], log_perm, high[:, 0]], axis=1))
    sat_pad = jnp.concatenate([low[:, 1], saturation, high[:, 1]], axis=1)
    trans_x, frac_x = face_pair(perm_pad[:, :-1], perm_pad[:, 1:], sat_pad[:, :-1], sat_pad[:, 1:])
    face_pos = lax.broadcasted_iota(jnp.int32, (slab_x + 1, 1, 1), 0)
    keep_face = jnp.where(
        face_pos == 0,
        slab_index > 0,
        jnp.where(face_pos == slab_x, slab_index < slab_count - 1, True),
    ).astype(jnp.float32)
    trans_x = trans_x * keep_face
    frac_x = frac_x * keep_face
    trans_y, frac_y, trans_z, frac_z = plane_faces(perm_pad[:, 1:-1], saturation)
    coeffs = (porosity / time_step, trans_x, frac_x, trans_y, frac_y, trans_z, frac_z)

    def planes(field):
        low = lax.ppermute(field[:, -1:], CELL, forward)
        high = lax.ppermute(field[:, :1], CELL, backward)
        return (low, high)

    def apply(vector, ghosts):
        padded = jnp.concatenate([ghosts[0], vector[:, 0], ghosts[1]], axis=1)
        out_pressure, out_water = operator(padded, vector[:, 1], coeffs)
        return jnp.stack([out_pressure, out_water], 1)

    def scale_planes(ghosts, scale):
        factor = scale[:, None, None, None]
        return (ghosts[0] / factor, ghosts[1] / factor)

    rhs_planes = (low[:, 2], high[:, 2])
    image = apply(rhs, rhs_planes)
    parts = jnp.stack([inner(rhs, rhs), inner(rhs, image)], 0)
    image_planes = planes(image[:, 0])
    reduced = cell_sum(parts)
    beta = jnp.sqrt(reduced[0] + epsilon)
    basis = [rhs / expand(beta)]
    basis_planes = [scale_planes(rhs_planes, beta)]
    image = image / expand(beta)
    image_planes = scale_planes(image_planes, beta)
    projected = [reduced[1] / (beta * beta)]
    columns = []
    for jdx in range(KRYLOV):
        ortho = image
        ortho_low, ortho_high = image_planes
        for idx in range(jdx + 1):
            ortho = ortho - expand(projected[idx]) * basis[idx]
            factor = projected[idx][:, None, None, None]
            ortho_low = ortho_low - factor * basis_planes[idx][0]
            ortho_high = ortho_high - factor * basis_planes[idx][1]
        ortho_planes = (ortho_low, ortho_high)
        if jdx == KRYLOV - 1:
            height = jnp.sqrt(cell_sum(inner(ortho, ortho)) + epsilon)
            columns.append(projected + [height])
            break
        image = apply(ortho, ortho_planes)
        parts = [inner(ortho, ortho)]
        parts += [inner(basis[idx], image) for idx in range(jdx + 1)]
        parts.append(inner(ortho, image))
        parts = jnp.stack(parts, 0)
        image_planes = planes(image[:, 0])
        reduced = cell_sum(parts)
        height = jnp.sqrt(reduced[0] + epsilon)
        columns.append(projected + [height])
        basis.append(ortho / expand(height))
        basis_planes.append(scale_planes(ortho_planes, height))
        image = image / expand(height)
        image_planes = scale_planes(image_planes, height)
        projected = [reduced[1 + idx] / height for idx in range(jdx + 1)]
        projected.append(reduced[jdx + 2] / (height * height))
    solved = least_squares(columns, beta)
    increment = expand(solved[0]) * basis[0]
    for jdx in range(1, KRYLOV):
        increment = increment + expand(solved[jdx]) * basis[jdx]
    cells = jnp.take(well_cell, obs_well)
    wells = well_cell.shape[0]
    component = (jnp.arange(obs_well.shape[0], dtype=jnp.int32) >= wells).astype(jnp.int32)
    slab_row = cells // plane - slab_index * slab_x
    inside = (slab_row >= 0) & (slab_row < slab_x)
    rows = 2 * slab_x * plane_rows
    row = component * (slab_x * plane_rows) + slab_row * plane_rows + (cells % plane) // plane_cols
    col_z = cells % plane_cols
    state = jnp.stack([pressure + increment[:, 0], saturation + increment[:, 1]], 1)
    table = state.reshape(local_members * rows, plane_cols)
    pick_z = (lax.broadcasted_iota(jnp.int32, (plane_cols, cells.shape[0]), 0) == col_z[None, :])
    by_row = jnp.dot(
        table,
        pick_z.astype(jnp.float32),
        precision=lax.Precision.HIGHEST,
        preferred_element_type=jnp.float32,
    )
    pick_row = (lax.broadcasted_iota(jnp.int32, (rows, cells.shape[0]), 0) == row[None, :]) & inside[None, :]
    picked = jnp.sum(
        by_row.reshape(local_members, rows, cells.shape[0]) * pick_row.astype(jnp.float32)[None],
        axis=1,
    )
    slab_pred = cell_sum(picked, doubling=True)
    predicted = lax.all_gather(slab_pred, "grp", axis=0, tiled=True)
    offset = lax.axis_index("grp") * local_members
    own_columns = ensemble_weights(predicted, obs_values, obs_error, noise, offset, local_members)
    scale_factor = 1.0 / math.sqrt(members - 1.0)

    def posterior_of(theta):
        flat = theta.reshape(local_members, cells_dev)
        update = jnp.dot(
            own_columns.T,
            lax.all_gather(flat * scale_factor, "grp", axis=0, tiled=True),
            precision=lax.Precision.HIGHEST,
            preferred_element_type=jnp.float32,
        )
        return (flat + update).reshape(theta.shape)

    return (increment, posterior_of(log_perm), posterior_of(porosity))


def split_mesh(mesh):
    devices = mesh.devices
    groups, slabs = devices.shape
    along_z = len({device.coords[2] for device in devices[0]})
    return Mesh(devices.reshape(groups, slabs // along_z, along_z), ("grp", "cy", "cz"))


def solution(mesh):
    mesh = split_mesh(mesh)
    in_specs = (
        P("grp", None, CELL, None, None),
        P("grp", CELL, None, None),
        P("grp", CELL, None, None),
        P("grp", CELL, None, None),
        P("grp", CELL, None, None),
        P(),
        P(),
        P(),
        P(),
        P(),
    )
    out_specs = (
        P("grp", None, CELL, None, None),
        P("grp", CELL, None, None),
        P("grp", CELL, None, None),
    )
    return jax.shard_map(local, mesh=mesh, in_specs=in_specs, out_specs=out_specs, check_vma=False)
```

```python
import math

import jax
import jax.numpy as jnp
from jax import lax
from jax.sharding import Mesh
from jax.sharding import PartitionSpec as P

KRYLOV = 4


epsilon = 1e-06
time_step = 0.1
compress = 0.5
inflation = 4.0


CELL = ("cy", "cz")


def cell_sum(values, doubling=False):
    for axis in ("cz", "cy"):
        size = lax.axis_size(axis)
        if not doubling or size & (size - 1):
            values = lax.psum(values, axis)
            continue
        step = 1
        while step < size:
            values = values + lax.ppermute(values, axis, [(i, i ^ step) for i in range(size)])
            step *= 2
    return values


def mobility(sat_field):
    return sat_field * sat_field + 0.5 * (1.0 - sat_field) * (1.0 - sat_field)


def face_pair(perm_low, perm_high, sat_low, sat_high):
    trans = (
        2.0
        * perm_low
        * perm_high
        / (perm_low + perm_high)
        * (0.5 * (mobility(sat_low) + mobility(sat_high)))
    )
    return (trans, trans * (0.5 * (sat_low + sat_high)))


def plane_faces(perm, sat_field):
    plane_rows = perm.shape[-2]
    plane_cols = perm.shape[-1]
    keep_rows = (
        lax.broadcasted_iota(jnp.int32, (plane_rows, plane_cols), 0) < plane_rows - 1
    ).astype(jnp.float32)
    keep_cols = (
        lax.broadcasted_iota(jnp.int32, (plane_rows, plane_cols), 1) < plane_cols - 1
    ).astype(jnp.float32)
    trans_y, frac_y = face_pair(
        perm, jnp.roll(perm, -1, -2), sat_field, jnp.roll(sat_field, -1, -2)
    )
    trans_z, frac_z = face_pair(
        perm, jnp.roll(perm, -1, -1), sat_field, jnp.roll(sat_field, -1, -1)
    )
    return (trans_y * keep_rows, frac_y * keep_rows, trans_z * keep_cols, frac_z * keep_cols)


def operator(padded, second, coeffs):
    accum, trans_x, frac_x, trans_y, frac_y, trans_z, frac_z = coeffs
    first = padded[..., 1:-1, :, :]
    diff_x = padded[..., 1:, :, :] - padded[..., :-1, :, :]
    diff_y = jnp.roll(first, -1, -2) - first
    diff_z = jnp.roll(first, -1, -1) - first

    def net(coef_x, coef_y, coef_z):
        flow_x = coef_x * diff_x
        flow_y = coef_y * diff_y
        flow_z = coef_z * diff_z
        return (
            flow_x[..., :-1, :, :]
            - flow_x[..., 1:, :, :]
            + (jnp.roll(flow_y, 1, -2) - flow_y)
            + (jnp.roll(flow_z, 1, -1) - flow_z)
        )

    out_pressure = accum * (compress * first + 0.5 * second) + net(trans_x, trans_y, trans_z)
    out_water = accum * second + net(frac_x, frac_y, frac_z)
    return (out_pressure, out_water)


def least_squares(columns, beta):
    rows = [list(column) for column in columns]
    cosines = []
    sines = []
    target = [beta] + [jnp.zeros_like(beta) for column in columns]
    for jdx in range(len(rows)):
        column = rows[jdx]
        for idx in range(jdx):
            upper = cosines[idx] * column[idx] + sines[idx] * column[idx + 1]
            column[idx + 1] = -sines[idx] * column[idx] + cosines[idx] * column[idx + 1]
            column[idx] = upper
        radius = jnp.sqrt(column[jdx] * column[jdx] + column[jdx + 1] * column[jdx + 1])
        cosines.append(column[jdx] / radius)
        sines.append(column[jdx + 1] / radius)
        column[jdx] = radius
        target[jdx + 1] = -sines[jdx] * target[jdx]
        target[jdx] = cosines[jdx] * target[jdx]
    count = len(rows)
    solved = [None] * count
    for jdx in reversed(range(count)):
        partial_sum = target[jdx]
        for idx in range(jdx + 1, count):
            partial_sum = partial_sum - rows[idx][jdx] * solved[idx]
        solved[jdx] = partial_sum / rows[jdx][jdx]
    return solved


def ensemble_weights(predicted, obs_values, obs_error, noise, offset, count):
    members = predicted.shape[0]
    sigma = math.sqrt(inflation) * obs_error
    center = jnp.mean(predicted, axis=0)
    spread = (predicted - center) / (math.sqrt(members - 1.0) * sigma)
    innov = (obs_values + sigma * noise - predicted) / sigma
    own_innov = lax.dynamic_slice_in_dim(innov, offset, count, 0)
    gram = jnp.eye(members, dtype=jnp.float32) + jnp.dot(
        spread, spread.T, precision=lax.Precision.HIGHEST, preferred_element_type=jnp.float32
    )
    cross = jnp.dot(
        spread, own_innov.T, precision=lax.Precision.HIGHEST, preferred_element_type=jnp.float32
    )
    factor = jnp.linalg.cholesky(gram)
    return jax.scipy.linalg.cho_solve((factor, True), cross)


def expand(values):
    return values[:, None, None, None, None]


def inner(left, right):
    return jnp.sum(left * right, axis=(1, 2, 3, 4))


def local(
    rhs, log_perm, porosity, saturation, pressure, obs_values, obs_error, noise, well_cell, obs_well
):
    local_members, slab_x, plane_rows, plane_cols = log_perm.shape
    members = noise.shape[0]
    plane = plane_rows * plane_cols
    cells_dev = slab_x * plane
    slab_index = lax.axis_index("cy") * lax.axis_size("cz") + lax.axis_index("cz")
    slab_count = lax.axis_size("cy") * lax.axis_size("cz")
    count = slab_count
    forward = [(i, i + 1) for i in range(count - 1)]
    backward = [(target, source) for source, target in forward]
    edges = (log_perm, saturation, rhs[:, 0])
    low = lax.ppermute(jnp.stack([field[:, -1:] for field in edges], 1), CELL, forward)
    high = lax.ppermute(jnp.stack([field[:, :1] for field in edges], 1), CELL, backward)
    perm_pad = jnp.exp(jnp.concatenate([low[:, 0], log_perm, high[:, 0]], axis=1))
    sat_pad = jnp.concatenate([low[:, 1], saturation, high[:, 1]], axis=1)
    trans_x, frac_x = face_pair(perm_pad[:, :-1], perm_pad[:, 1:], sat_pad[:, :-1], sat_pad[:, 1:])
    face_pos = lax.broadcasted_iota(jnp.int32, (slab_x + 1, 1, 1), 0)
    keep_face = jnp.where(
        face_pos == 0,
        slab_index > 0,
        jnp.where(face_pos == slab_x, slab_index < slab_count - 1, True),
    ).astype(jnp.float32)
    trans_x = trans_x * keep_face
    frac_x = frac_x * keep_face
    trans_y, frac_y, trans_z, frac_z = plane_faces(perm_pad[:, 1:-1], saturation)
    coeffs = (porosity / time_step, trans_x, frac_x, trans_y, frac_y, trans_z, frac_z)

    def planes(field):
        low = lax.ppermute(field[:, -1:], CELL, forward)
        high = lax.ppermute(field[:, :1], CELL, backward)
        return (low, high)

    def apply(vector, ghosts):
        padded = jnp.concatenate([ghosts[0], vector[:, 0], ghosts[1]], axis=1)
        out_pressure, out_water = operator(padded, vector[:, 1], coeffs)
        return jnp.stack([out_pressure, out_water], 1)

    def scale_planes(ghosts, scale):
        factor = scale[:, None, None, None]
        return (ghosts[0] / factor, ghosts[1] / factor)

    rhs_planes = (low[:, 2], high[:, 2])
    image = apply(rhs, rhs_planes)
    parts = jnp.stack([inner(rhs, rhs), inner(rhs, image)], 0)
    image_planes = planes(image[:, 0])
    reduced = cell_sum(parts)
    beta = jnp.sqrt(reduced[0] + epsilon)
    basis = [rhs / expand(beta)]
    basis_planes = [scale_planes(rhs_planes, beta)]
    image = image / expand(beta)
    image_planes = scale_planes(image_planes, beta)
    projected = [reduced[1] / (beta * beta)]
    columns = []
    for jdx in range(KRYLOV):
        ortho = image
        ortho_low, ortho_high = image_planes
        for idx in range(jdx + 1):
            ortho = ortho - expand(projected[idx]) * basis[idx]
            factor = projected[idx][:, None, None, None]
            ortho_low = ortho_low - factor * basis_planes[idx][0]
            ortho_high = ortho_high - factor * basis_planes[idx][1]
        ortho_planes = (ortho_low, ortho_high)
        if jdx == KRYLOV - 1:
            height = jnp.sqrt(cell_sum(inner(ortho, ortho)) + epsilon)
            columns.append(projected + [height])
            break
        image = apply(ortho, ortho_planes)
        parts = [inner(ortho, ortho)]
        parts += [inner(basis[idx], image) for idx in range(jdx + 1)]
        parts.append(inner(ortho, image))
        parts = jnp.stack(parts, 0)
        image_planes = planes(image[:, 0])
        reduced = cell_sum(parts)
        height = jnp.sqrt(reduced[0] + epsilon)
        columns.append(projected + [height])
        basis.append(ortho / expand(height))
        basis_planes.append(scale_planes(ortho_planes, height))
        image = image / expand(height)
        image_planes = scale_planes(image_planes, height)
        projected = [reduced[1 + idx] / height for idx in range(jdx + 1)]
        projected.append(reduced[jdx + 2] / (height * height))
    solved = least_squares(columns, beta)
    increment = expand(solved[0]) * basis[0]
    for jdx in range(1, KRYLOV):
        increment = increment + expand(solved[jdx]) * basis[jdx]
    cells = jnp.take(well_cell, obs_well)
    wells = well_cell.shape[0]
    component = (jnp.arange(obs_well.shape[0], dtype=jnp.int32) >= wells).astype(jnp.int32)
    slab_row = cells // plane - slab_index * slab_x
    inside = (slab_row >= 0) & (slab_row < slab_x)
    rows = 2 * slab_x * plane_rows
    row = component * (slab_x * plane_rows) + slab_row * plane_rows + (cells % plane) // plane_cols
    col_z = cells % plane_cols
    state = jnp.stack([pressure + increment[:, 0], saturation + increment[:, 1]], 1)
    table = state.reshape(local_members * rows, plane_cols)
    pick_z = (lax.broadcasted_iota(jnp.int32, (plane_cols, cells.shape[0]), 0) == col_z[None, :])
    by_row = jnp.dot(
        table,
        pick_z.astype(jnp.float32),
        precision=lax.Precision.HIGHEST,
        preferred_element_type=jnp.float32,
    )
    pick_row = (lax.broadcasted_iota(jnp.int32, (rows, cells.shape[0]), 0) == row[None, :]) & inside[None, :]
    picked = jnp.sum(
        by_row.reshape(local_members, rows, cells.shape[0]) * pick_row.astype(jnp.float32)[None],
        axis=1,
    )
    slab_pred = cell_sum(picked, doubling=True)
    predicted = slab_pred
    group = lax.axis_index("grp")
    step = 1
    while step < lax.axis_size("grp"):
        other = lax.ppermute(predicted, "grp", [(i, i ^ step) for i in range(lax.axis_size("grp"))])
        predicted = jnp.where(
            (group & step) == 0,
            jnp.concatenate([predicted, other], 0),
            jnp.concatenate([other, predicted], 0),
        )
        step *= 2
    params = jnp.stack([log_perm, porosity], 1).reshape(local_members, 2 * cells_dev)
    offset = lax.axis_index("grp") * local_members
    own_columns = ensemble_weights(predicted, obs_values, obs_error, noise, offset, local_members)
    scale_factor = 1.0 / math.sqrt(members - 1.0)
    scaled = params * scale_factor
    update = jnp.dot(
        own_columns.T,
        lax.all_gather(scaled, "grp", axis=0, tiled=True),
        precision=lax.Precision.HIGHEST,
        preferred_element_type=jnp.float32,
    )
    posterior = params + update
    posterior = posterior.reshape(local_members, 2, slab_x, plane_rows, plane_cols)
    return (increment, posterior[:, 0], posterior[:, 1])


def split_mesh(mesh):
    devices = mesh.devices
    groups, slabs = devices.shape
    along_z = len({device.coords[2] for device in devices[0]})
    return Mesh(devices.reshape(groups, slabs // along_z, along_z), ("grp", "cy", "cz"))


def solution(mesh):
    mesh = split_mesh(mesh)
    in_specs = (
        P("grp", None, CELL, None, None),
        P("grp", CELL, None, None),
        P("grp", CELL, None, None),
        P("grp", CELL, None, None),
        P("grp", CELL, None, None),
        P(),
        P(),
        P(),
        P(),
        P(),
    )
    out_specs = (
        P("grp", None, CELL, None, None),
        P("grp", CELL, None, None),
        P("grp", CELL, None, None),
    )
    return jax.shard_map(local, mesh=mesh, in_specs=in_specs, out_specs=out_specs, check_vma=False)
```
